32 devices in a mesh: tm: 8 (over z, y), col: 4 (over x, core).
Axes of the slice: x: 2, y: 2, z: 4, core: 2. Of those that a mesh axis runs over, the one named last changes fastest.
Arguments:
- observed: bfloat16 [16, 128, 512], P('tm', None, 'col'), may hold values from -6 to 6
- input_gain: float32 [512], P('col'), may hold values from 0.03 to 0.3
- persist: float32 [16, 512], P('tm', 'col'), may hold values from 0.5 to 1, as said below
- coupling: bfloat16 [16, 512, 512], P('tm', None, 'col'), may hold values from -0.02734375 to 0.02734375
- pattern: int32 [8, 8], replicated, may hold values 0 or 1
Outputs:
- filtered: float32 [16, 128, 512], P('tm', None, 'col')
- smoothed: float32 [16, 128, 512], P('tm', None, 'col')
The draws below stay inside these ranges and needn't reach their ends.
Inputs may be any that keep to these rules, and one draw needn't show every extreme that they name: `persist`: persistence of each state component at each step.
All inputs are finite; a program needn't handle non-finite values.
Results may differ from the reference program's by a relative error of at most 0.0003.
Values may be sent and summed in bfloat16 or wider, within the bound.
No kernel may reach another device: no remote copies, remote signals or barrier semaphores. Data moves between devices by JAX's collectives and lax.ppermute only.
A program may use at most 64 MiB of HBM per device.

```python
import math
import jax
import jax.numpy as jnp
from jax import lax

S = 512
BLK = 64
NB = 8
B = 128
STEPS_DEV = 2
WINDOW_STEPS = 16


def draw_persist(key, part):
    key_rate, key_spread, key_when = jax.random.split(key, 3)
    low_log, high_log = (math.log(0.0001), math.log(0.05))
    rates = jnp.exp(jax.random.uniform(key_rate, (S,), jnp.float32, low_log, high_log))
    spread = jnp.exp(jax.random.uniform(key_spread, (WINDOW_STEPS // STEPS_DEV, S), jnp.float32, -0.7, 0.7))
    spread = jnp.repeat(spread, STEPS_DEV, axis=0)
    state_moments = jax.random.randint(key_when, (4,), 0, WINDOW_STEPS)
    noise_pulses = jnp.any(jnp.arange(WINDOW_STEPS)[:, None] == state_moments[None, :], axis=1)
    kept_entries = jnp.exp(-rates[None, :] * spread)
    return jnp.where(noise_pulses[:, None], 0.6 * kept_entries, kept_entries).astype(jnp.float32)


def touch_ends(values, own_key, least, largest):
    extent = values.shape
    index_at = [jax.random.randint(jax.random.fold_in(own_key, axis), (), 0, extent[axis]) for axis in range(len(extent))]
    values = values.at[tuple(index_at)].set(least)
    longest = extent.index(max(extent))
    index_at[longest] = (index_at[longest] + 1) % extent[longest]
    return values.at[tuple(index_at)].set(largest)


def steps_of(stream_key, shape, pieces, least, largest):
    loudness = 1.0
    for dim, parts in pieces:
        draws = jax.random.uniform(jax.random.fold_in(jax.random.fold_in(stream_key, 6), dim), (parts,), jnp.float32, least / len(pieces), largest / len(pieces))
        loudness = loudness * jnp.repeat(jnp.exp(draws), shape[dim] // parts).reshape((-1,) + (1,) * (len(shape) - 1 - dim))
    return loudness


def centred(stream_key, extent, width, reach, shards=(), dtype=jnp.bfloat16):
    factor_of = steps_of(stream_key, extent, shards, -0.22, 0.18) if shards else 1.0
    values = jax.random.normal(stream_key, extent, jnp.float32) * width * factor_of
    return jnp.minimum(jnp.maximum(values, -reach), reach).astype(dtype)


def setup_inputs(seed: int = 0) -> dict:
    seeds = jax.random.split(jax.random.key(seed), 6)
    observed = centred(seeds[0], (WINDOW_STEPS, B, S), 1.0, 6.0, ((0, 8), (2, 4)))
    input_gain = jnp.clip(jnp.exp(math.log(0.3) - 2.3025852 * jax.random.uniform(seeds[1], (S,), jnp.float32) ** steps_of(seeds[1], (S,), ((0, 4),), -0.2, 0.2)), 0.03, 0.3)
    persist = draw_persist(jax.random.fold_in(seeds[5], 71), 0)
    coupling = centred(seeds[3], (WINDOW_STEPS, S, S), (0.04 / S ** 0.5), 0.02734375, ((0, 8), (2, 4)))
    pattern = touch_ends((jax.random.randint(seeds[4], (NB, NB), 0, 2) < 1).astype(jnp.int32), jax.random.fold_in(seeds[4], 1), 0, 1)
    return dict(observed=observed, input_gain=input_gain, persist=persist, coupling=coupling, pattern=pattern)


def expand(pattern):
    return jnp.repeat(jnp.repeat(pattern.astype(jnp.float32), BLK, axis=0), BLK, axis=1)


def reference(observed, input_gain, persist, coupling, pattern):
    mask_full = expand(pattern)

    def transition(weights, diagonal):
        return weights.astype(jnp.float32) * mask_full + jnp.diag(diagonal)

    def forward(x, inputs_now):
        seen, weights, diagonal = inputs_now
        matrix = transition(weights, diagonal)
        x = jnp.dot(x, matrix, precision=lax.Precision.HIGHEST, preferred_element_type=jnp.float32) + input_gain[None, :] * seen.astype(jnp.float32)
        return x, x

    start_state = jnp.zeros((observed.shape[1], observed.shape[2]), jnp.float32)
    _, filtered = lax.scan(forward, start_state, (observed, coupling, persist))

    def backward(s, inputs_now):
        x, weights, diagonal = inputs_now
        matrix = transition(weights, diagonal)
        residual = s - jnp.dot(x, matrix, precision=lax.Precision.HIGHEST, preferred_element_type=jnp.float32)
        s = x + jnp.dot(residual, matrix.T, precision=lax.Precision.HIGHEST, preferred_element_type=jnp.float32)
        return s, s

    final_state = filtered[-1]
    _, prior_values = lax.scan(backward, final_state, (filtered[:-1], coupling[1:], persist[1:]), reverse=True)
    smoothed = jnp.concatenate([prior_values, final_state[None]], axis=0)
    return filtered, smoothed
```

```python
import jax
import jax.numpy as jnp
from jax import lax
from jax.sharding import PartitionSpec as P


def passed_along(shard, axis, by):
    length = lax.axis_size(axis)
    pairs = [(i, i + by) for i in range(length) if 0 <= i + by < length]
    return lax.ppermute(shard, axis, pairs)


def split_dot(state, weights, transposed):
    high = state.astype(jnp.bfloat16)
    low = (state - high.astype(jnp.float32)).astype(jnp.bfloat16)
    both = jnp.concatenate([high, low], axis=0)
    contract = 1 if transposed else 0
    prod = lax.dot_general(
        both, weights, (((1,), (contract,)), ((), ())), preferred_element_type=jnp.float32
    )
    rows = state.shape[0]
    return prod[:rows] + prod[rows:]


def local(observed, input_gain, persist, coupling, pattern):
    step_count = observed.shape[0]
    state_width = coupling.shape[1]
    block_count = pattern.shape[0]
    block_size = state_width // block_count
    time_groups = lax.axis_size("tm")

    full_coupling = lax.all_gather(coupling, "col", axis=2, tiled=True)
    small = jnp.concatenate([persist, input_gain[None]], axis=0)
    small = lax.all_gather(small, "col", axis=1, tiled=True)
    diag = small[:step_count]
    gain = small[step_count]
    seen = lax.all_to_all(observed, "col", split_axis=1, concat_axis=2, tiled=True)

    mask = jnp.broadcast_to(
        pattern.astype(jnp.bfloat16)[:, None, :, None],
        (block_count, block_size, block_count, block_size),
    ).reshape(state_width, state_width)
    weights = full_coupling * mask[None]
    driven = gain[None, None, :] * seen.astype(jnp.float32)

    def forward(x):
        out = []
        for k in range(step_count):
            x = split_dot(x, weights[k], False) + x * diag[k][None] + driven[k]
            out.append(x)
        return out

    def backward(e):
        out = [None] * step_count
        out[step_count - 1] = e
        for k in range(step_count - 1, -1, -1):
            w = e + driven[k]
            e = split_dot(w, weights[k], True) + w * diag[k][None]
            if k > 0:
                out[k - 1] = e
        return out, e

    def stage(carry):
        x_in, e_in = carry
        xs = forward(x_in)
        _, e_out = backward(e_in)
        return passed_along(xs[-1], "tm", 1), passed_along(e_out, "tm", -1)

    zeros = jnp.zeros(driven.shape[1:], jnp.float32)
    carry = (zeros, zeros)
    if time_groups <= 8:
        for _ in range(time_groups - 1):
            carry = stage(carry)
    else:
        carry = lax.fori_loop(0, time_groups - 1, lambda _, c: stage(c), carry)
    x_in, e_in = carry
    xs = forward(x_in)
    es, _ = backward(e_in)
    filtered = jnp.stack(xs)
    smoothed = jnp.stack([x + e for x, e in zip(xs, es)])
    both = jnp.stack([filtered, smoothed])
    both = lax.all_to_all(both, "col", split_axis=3, concat_axis=2, tiled=True)
    return both[0], both[1]


def solution(mesh):
    return jax.shard_map(
        local,
        mesh=mesh,
        in_specs=(P("tm", None, "col"), P("col"), P("tm", "col"), P("tm", None, "col"), P()),
        out_specs=(P("tm", None, "col"), P("tm", None, "col")),
        check_vma=False,
    )
```

```python
import jax
import jax.numpy as jnp
from jax import lax
from jax.sharding import PartitionSpec as P


def passed_along(shard, axis, by):
    length = lax.axis_size(axis)
    pairs = [(i, i + by) for i in range(length) if 0 <= i + by < length]
    return lax.ppermute(shard, axis, pairs)


def bf16_part(value):
    return lax.reduce_precision(value, exponent_bits=8, mantissa_bits=7)


def split_dot(state, weights, transposed):
    high = bf16_part(state)
    low = state - high
    both = jnp.concatenate([high, low], axis=0).astype(jnp.bfloat16)
    contract = 1 if transposed else 0
    prod = lax.dot_general(
        both, weights, (((1,), (contract,)), ((), ())), preferred_element_type=jnp.float32
    )
    rows = state.shape[0]
    return prod[:rows] + prod[rows:]


def three_pieces(value):
    high = bf16_part(value)
    rest = value - high
    mid = bf16_part(rest)
    return jnp.stack([high, mid, rest - mid]).astype(jnp.bfloat16)


def local(observed, input_gain, persist, coupling, pattern):
    step_count, rows, cols = observed.shape
    state_width = coupling.shape[1]
    block_count = pattern.shape[0]
    block_size = state_width // block_count
    time_groups = lax.axis_size("tm")
    col_groups = lax.axis_size("col")
    own_rows = rows // col_groups

    small = jnp.concatenate([persist, input_gain[None]], axis=0)
    small_pieces = three_pieces(small).reshape(-1)
    coupling_flat = coupling.reshape(-1)
    seen_parts = observed.reshape(step_count, col_groups, own_rows, cols).transpose(1, 0, 2, 3)
    packet = jnp.concatenate(
        [
            jnp.broadcast_to(coupling_flat[None], (col_groups,) + coupling_flat.shape),
            seen_parts.reshape(col_groups, -1),
            jnp.broadcast_to(small_pieces[None], (col_groups,) + small_pieces.shape),
        ],
        axis=1,
    )
    packet = lax.all_to_all(packet, "col", split_axis=0, concat_axis=0, tiled=True)
    n_coupling = coupling_flat.shape[0]
    n_seen = step_count * own_rows * cols
    full_coupling = (
        packet[:, :n_coupling]
        .reshape(col_groups, step_count, state_width, cols)
        .transpose(1, 2, 0, 3)
        .reshape(step_count, state_width, state_width)
    )
    seen = (
        packet[:, n_coupling : n_coupling + n_seen]
        .reshape(col_groups, step_count, own_rows, cols)
        .transpose(1, 2, 0, 3)
        .reshape(step_count, own_rows, state_width)
    )
    small = (
        packet[:, n_coupling + n_seen :]
        .astype(jnp.float32)
        .reshape(col_groups, 3, step_count + 1, cols)
    )
    small = (small[:, 0] + small[:, 1] + small[:, 2]).transpose(1, 0, 2).reshape(step_count + 1, state_width)
    diag = small[:step_count]
    gain = small[step_count]

    mask = jnp.broadcast_to(
        pattern.astype(jnp.bfloat16)[:, None, :, None],
        (block_count, block_size, block_count, block_size),
    ).reshape(state_width, state_width)
    weights = full_coupling * mask[None]
    driven = gain[None, None, :] * seen.astype(jnp.float32)

    def forward(x):
        out = []
        for k in range(step_count):
            x = split_dot(x, weights[k], False) + x * diag[k][None] + driven[k]
            out.append(x)
        return out

    def backward(e):
        out = [None] * step_count
        out[step_count - 1] = e
        for k in range(step_count - 1, -1, -1):
            w = e + driven[k]
            e = split_dot(w, weights[k], True) + w * diag[k][None]
            if k > 0:
                out[k - 1] = e
        return out, e

    def stage(carry):
        x_in, e_in = carry
        xs = forward(x_in)
        _, e_out = backward(e_in)
        x_out, e_out = lax.optimization_barrier((xs[-1], e_out))
        sent = (passed_along(x_out, "tm", 1), passed_along(e_out, "tm", -1))
        return lax.optimization_barrier(sent)

    zeros = jnp.zeros(driven.shape[1:], jnp.float32)
    carry = (zeros, zeros)
    if time_groups <= 8:
        for _ in range(time_groups - 1):
            carry = stage(carry)
    else:
        carry = lax.fori_loop(0, time_groups - 1, lambda _, c: stage(c), carry)
    x_in, e_in = carry
    xs = forward(x_in)
    es, _ = backward(e_in)
    filtered = jnp.stack(xs)
    smoothed = jnp.stack([x + e for x, e in zip(xs, es)])
    both = jnp.stack([filtered, smoothed])
    both = both.reshape(2, step_count, own_rows, col_groups, cols).transpose(3, 0, 1, 2, 4)
    both = lax.all_to_all(both, "col", split_axis=0, concat_axis=0, tiled=True)
    both = both.transpose(1, 2, 0, 3, 4).reshape(2, step_count, rows, cols)
    return both[0], both[1]


def solution(mesh):
    return jax.shard_map(
        local,
        mesh=mesh,
        in_specs=(P("tm", None, "col"), P("col"), P("tm", "col"), P("tm", None, "col"), P()),
        out_specs=(P("tm", None, "col"), P("tm", None, "col")),
        check_vma=False,
    )
```

```python
import jax
import jax.numpy as jnp
from jax import lax
from jax.sharding import PartitionSpec as P


def bf16_part(value):
    return lax.reduce_precision(value, exponent_bits=8, mantissa_bits=7)


def split_dot(state, weights):
    high = bf16_part(state)
    low = state - high
    both = jnp.concatenate([high, low], axis=0).astype(jnp.bfloat16)
    prod = jnp.dot(both, weights, preferred_element_type=jnp.float32)
    rows = state.shape[0]
    return prod[:rows] + prod[rows:]


def three_pieces(value):
    high = bf16_part(value)
    rest = value - high
    mid = bf16_part(rest)
    return jnp.stack([high, mid, rest - mid]).astype(jnp.bfloat16)


def local(observed, input_gain, persist, coupling, pattern):
    step_count, rows, cols = observed.shape
    state_width = coupling.shape[1]
    block_count = pattern.shape[0]
    block_size = state_width // block_count
    time_groups = lax.axis_size("tm")
    col_groups = lax.axis_size("col")
    half = col_groups // 2
    own_rows = rows // half
    col_pos = lax.axis_index("col")
    backward = col_pos >= half

    small = jnp.concatenate([persist, input_gain[None]], axis=0)
    small_rows = 3 * (step_count + 1)
    small_pad = -small_rows % 16
    small_pieces = jnp.pad(three_pieces(small).reshape(small_rows, cols), ((0, small_pad), (0, 0)))
    coupling_rows = coupling.reshape(step_count * state_width, cols)
    seen_parts = observed.reshape(step_count, half, own_rows, cols).transpose(1, 0, 2, 3)
    seen_parts = seen_parts.reshape(half, step_count * own_rows, cols)
    seen_parts = jnp.concatenate([seen_parts] * (col_groups // half), axis=0)
    packet = jnp.concatenate(
        [
            jnp.broadcast_to(coupling_rows[None], (col_groups,) + coupling_rows.shape),
            seen_parts,
            jnp.broadcast_to(small_pieces[None], (col_groups,) + small_pieces.shape),
        ],
        axis=1,
    )
    packet = lax.all_to_all(packet, "col", split_axis=0, concat_axis=0, tiled=True)
    n_coupling = step_count * state_width
    n_seen = step_count * own_rows
    blocks = packet[:, :n_coupling].reshape(col_groups, step_count, state_width, cols)
    straight = blocks.transpose(1, 2, 0, 3).reshape(step_count, state_width, state_width)
    turned = blocks.transpose(1, 0, 3, 2).reshape(step_count, state_width, state_width)[::-1]
    pattern_used = jnp.where(backward, pattern.T, pattern).astype(jnp.bfloat16)
    mask = jnp.broadcast_to(
        pattern_used[:, None, :, None],
        (block_count, block_size, block_count, block_size),
    ).reshape(state_width, state_width)
    weights = jnp.where(backward, turned, straight) * mask[None]

    seen = (
        packet[:, n_coupling : n_coupling + n_seen]
        .reshape(col_groups, step_count, own_rows, cols)
        .transpose(1, 2, 0, 3)
        .reshape(step_count, own_rows, state_width)
    )
    small = packet[:, n_coupling + n_seen : n_coupling + n_seen + small_rows].astype(jnp.float32)
    small = small.reshape(col_groups, 3, step_count + 1, cols)
    small = (small[:, 0] + small[:, 1] + small[:, 2]).transpose(1, 0, 2)
    small = small.reshape(step_count + 1, state_width)
    diag = small[:step_count]
    gain = small[step_count]
    driven = gain[None, None, :] * seen.astype(jnp.float32)

    zeros = jnp.zeros_like(driven)
    before = jnp.where(backward, driven[::-1], zeros)
    after = jnp.where(backward, zeros, driven)
    diag = jnp.where(backward, diag[::-1], diag)

    def chain(y):
        out = []
        for k in range(step_count):
            z = y + before[k]
            y = split_dot(z, weights[k]) + z * diag[k][None] + after[k]
            out.append(y)
        return out

    pairs = []
    for t in range(time_groups):
        for c in range(col_groups):
            to = t + (-1 if c >= half else 1)
            if 0 <= to < time_groups:
                pairs.append((t * col_groups + c, to * col_groups + c))

    def stage(y):
        return lax.ppermute(chain(y)[-1], ("tm", "col"), pairs)

    y = jnp.zeros(driven.shape[1:], jnp.float32)
    if time_groups <= 8:
        for _ in range(time_groups - 1):
            y = stage(y)
    else:
        y = lax.fori_loop(0, time_groups - 1, lambda _, c: stage(c), y)
    ys = chain(y)
    mine = jnp.where(backward, jnp.stack([ys[0], y]), jnp.stack(ys))
    mine = mine.reshape(step_count, own_rows, col_groups, cols).transpose(2, 0, 1, 3)
    got = lax.all_to_all(mine, "col", split_axis=0, concat_axis=0, tiled=True)
    got = got.reshape(2, half, step_count, own_rows, cols).transpose(0, 2, 1, 3, 4)
    got = got.reshape(2, step_count, rows, cols)
    filtered = got[0]
    return filtered, filtered + got[1]


def solution(mesh):
    return jax.shard_map(
        local,
        mesh=mesh,
        in_specs=(P("tm", None, "col"), P("col"), P("tm", "col"), P("tm", None, "col"), P()),
        out_specs=(P("tm", None, "col"), P("tm", None, "col")),
        check_vma=False,
    )
```

```python
import jax
import jax.numpy as jnp
from jax import lax
from jax.sharding import PartitionSpec as P


def bf16_part(value):
    return lax.reduce_precision(value, exponent_bits=8, mantissa_bits=7)


def split_dot(state, weights):
    high = bf16_part(state)
    low = state - high
    both = jnp.concatenate([high, low], axis=0).astype(jnp.bfloat16)
    prod = jnp.dot(both, weights, preferred_element_type=jnp.float32)
    rows = state.shape[0]
    return prod[:rows] + prod[rows:]


def three_pieces(value):
    high = bf16_part(value)
    rest = value - high
    mid = bf16_part(rest)
    return jnp.stack([high, mid, rest - mid]).astype(jnp.bfloat16)


def local(observed, input_gain, persist, coupling, pattern):
    step_count, rows, cols = observed.shape
    state_width = coupling.shape[1]
    block_count = pattern.shape[0]
    block_size = state_width // block_count
    time_groups = lax.axis_size("tm")
    col_groups = lax.axis_size("col")
    half = col_groups // 2
    own_rows = rows // half
    col_pos = lax.axis_index("col")
    backward = col_pos >= half

    small = jnp.concatenate([persist, input_gain[None]], axis=0)
    small_rows = 3 * (step_count + 1)
    small_pad = -small_rows % 16
    small_pieces = jnp.pad(three_pieces(small).reshape(small_rows, cols), ((0, small_pad), (0, 0)))
    coupling_rows = coupling.reshape(step_count * state_width, cols)
    seen_parts = observed.reshape(step_count, half, own_rows, cols).transpose(1, 0, 2, 3)
    seen_parts = seen_parts.reshape(half, step_count * own_rows, cols)
    seen_parts = jnp.concatenate([seen_parts] * (col_groups // half), axis=0)
    packet = jnp.concatenate(
        [
            jnp.broadcast_to(coupling_rows[None], (col_groups,) + coupling_rows.shape),
            seen_parts,
            jnp.broadcast_to(small_pieces[None], (col_groups,) + small_pieces.shape),
        ],
        axis=1,
    )
    packet = lax.all_to_all(packet, "col", split_axis=0, concat_axis=0, tiled=True)
    n_coupling = step_count * state_width
    n_seen = step_count * own_rows
    blocks = packet[:, :n_coupling].reshape(col_groups, step_count, state_width, cols)
    def expanded(bits):
        return jnp.broadcast_to(
            bits.astype(jnp.bfloat16)[:, None, :, None],
            (block_count, block_size, block_count, block_size),
        ).reshape(state_width, state_width)

    def straight(b):
        full = b.transpose(1, 2, 0, 3).reshape(step_count, state_width, state_width)
        return full * expanded(pattern)[None]

    def turned(b):
        full = b.transpose(1, 0, 3, 2).reshape(step_count, state_width, state_width)
        return full[::-1] * expanded(pattern.T)[None]

    weights = lax.cond(backward, turned, straight, blocks)

    seen = (
        packet[:, n_coupling : n_coupling + n_seen]
        .reshape(col_groups, step_count, own_rows, cols)
        .transpose(1, 2, 0, 3)
        .reshape(step_count, own_rows, state_width)
    )
    small = packet[:, n_coupling + n_seen : n_coupling + n_seen + small_rows].astype(jnp.float32)
    small = small.reshape(col_groups, 3, step_count + 1, cols)
    small = (small[:, 0] + small[:, 1] + small[:, 2]).transpose(1, 0, 2)
    small = small.reshape(step_count + 1, state_width)
    diag = small[:step_count]
    gain = small[step_count]
    driven = gain[None, None, :] * seen.astype(jnp.float32)

    zeros = jnp.zeros_like(driven)
    before = jnp.where(backward, driven[::-1], zeros)
    after = jnp.where(backward, zeros, driven)
    diag = jnp.where(backward, diag[::-1], diag)

    def chain(y):
        out = []
        for k in range(step_count):
            z = y + before[k]
            y = split_dot(z, weights[k]) + z * diag[k][None] + after[k]
            out.append(y)
        return out

    pairs = []
    for t in range(time_groups):
        for c in range(col_groups):
            to = t + (-1 if c >= half else 1)
            if 0 <= to < time_groups:
                pairs.append((t * col_groups + c, to * col_groups + c))

    def stage(y):
        return lax.ppermute(chain(y)[-1], ("tm", "col"), pairs)

    y = jnp.zeros(driven.shape[1:], jnp.float32)
    if time_groups <= 8:
        for _ in range(time_groups - 1):
            y = stage(y)
    else:
        y = lax.fori_loop(0, time_groups - 1, lambda _, c: stage(c), y)
    ys = chain(y)
    mine = jnp.where(backward, jnp.stack([ys[0], y]), jnp.stack(ys))
    mine = mine.reshape(step_count, own_rows, col_groups, cols).transpose(2, 0, 1, 3)
    got = lax.all_to_all(mine, "col", split_axis=0, concat_axis=0, tiled=True)
    got = got.reshape(2, half, step_count, own_rows, cols).transpose(0, 2, 1, 3, 4)
    got = got.reshape(2, step_count, rows, cols)
    filtered = got[0]
    return filtered, filtered + got[1]


def solution(mesh):
    return jax.shard_map(
        local,
        mesh=mesh,
        in_specs=(P("tm", None, "col"), P("col"), P("tm", "col"), P("tm", None, "col"), P()),
        out_specs=(P("tm", None, "col"), P("tm", None, "col")),
        check_vma=False,
    )
```

```python
import jax
import jax.numpy as jnp
from jax import lax
from jax.sharding import PartitionSpec as P


def bf16_part(value):
    return lax.reduce_precision(value, exponent_bits=8, mantissa_bits=7)


def split_dot(state, weights, transposed):
    high = bf16_part(state)
    low = state - high
    both = jnp.concatenate([high, low], axis=0).astype(jnp.bfloat16)
    contract = 1 if transposed else 0
    prod = lax.dot_general(
        both, weights, (((1,), (contract,)), ((), ())), preferred_element_type=jnp.float32
    )
    rows = state.shape[0]
    return prod[:rows] + prod[rows:]


def three_pieces(value):
    high = bf16_part(value)
    rest = value - high
    mid = bf16_part(rest)
    return jnp.stack([high, mid, rest - mid]).astype(jnp.bfloat16)


def passed_along(shard, axis, by):
    length = lax.axis_size(axis)
    pairs = [(i, i + by) for i in range(length) if 0 <= i + by < length]
    return lax.ppermute(shard, axis, pairs)


def local(observed, input_gain, persist, coupling, pattern):
    step_count, rows, cols = observed.shape
    state_width = coupling.shape[1]
    block_count = pattern.shape[0]
    block_size = state_width // block_count
    time_groups = lax.axis_size("tm")
    col_groups = lax.axis_size("col")
    own_rows = rows // col_groups
    tm_pos = lax.axis_index("tm")

    small = jnp.concatenate([persist, input_gain[None]], axis=0)
    small_rows = 3 * (step_count + 1)
    small_pad = -small_rows % 16
    small_pieces = jnp.pad(three_pieces(small).reshape(small_rows, cols), ((0, small_pad), (0, 0)))
    coupling_rows = coupling.reshape(step_count * state_width, cols)
    seen_parts = observed.reshape(step_count, col_groups, own_rows, cols).transpose(1, 0, 2, 3)
    seen_parts = seen_parts.reshape(col_groups, step_count * own_rows, cols)
    packet = jnp.concatenate(
        [
            jnp.broadcast_to(coupling_rows[None], (col_groups,) + coupling_rows.shape),
            seen_parts,
            jnp.broadcast_to(small_pieces[None], (col_groups,) + small_pieces.shape),
        ],
        axis=1,
    )
    packet = lax.all_to_all(packet, "col", split_axis=0, concat_axis=0, tiled=True)
    n_coupling = step_count * state_width
    n_seen = step_count * own_rows
    mask = jnp.broadcast_to(
        pattern.astype(jnp.bfloat16)[:, None, :, None],
        (block_count, block_size, block_count, block_size),
    ).reshape(state_width, state_width)
    weights = (
        packet[:, :n_coupling]
        .reshape(col_groups, step_count, state_width, cols)
        .transpose(1, 2, 0, 3)
        .reshape(step_count, state_width, state_width)
    ) * mask[None]
    seen = (
        packet[:, n_coupling : n_coupling + n_seen]
        .reshape(col_groups, step_count, own_rows, cols)
        .transpose(1, 2, 0, 3)
        .reshape(step_count, own_rows, state_width)
    )
    small = packet[:, n_coupling + n_seen : n_coupling + n_seen + small_rows].astype(jnp.float32)
    small = small.reshape(col_groups, 3, step_count + 1, cols)
    small = (small[:, 0] + small[:, 1] + small[:, 2]).transpose(1, 0, 2)
    small = small.reshape(step_count + 1, state_width)
    diag = small[:step_count]
    gain = small[step_count]
    driven = gain[None, None, :] * seen.astype(jnp.float32)

    def forward(x):
        out = []
        for k in range(step_count):
            x = split_dot(x, weights[k], False) + x * diag[k][None] + driven[k]
            out.append(x)
        return out

    def backward(e):
        out = []
        for k in range(step_count - 1, -1, -1):
            w = e + driven[k]
            e = split_dot(w, weights[k], True) + w * diag[k][None]
            out.append(e)
        return out

    zeros = jnp.zeros(driven.shape[1:], jnp.float32)
    x_in, e_in = zeros, zeros
    if time_groups <= 8 and time_groups % 2 == 0:
        last = time_groups - 1
        for k in range(last):
            xs = forward(x_in)
            es = backward(e_in)
            send = jnp.where(tm_pos == k, xs[-1], es[-1])
            pairs = [(k * col_groups + c, (k + 1) * col_groups + c) for c in range(col_groups)]
            pairs += [((last - k) * col_groups + c, (last - k - 1) * col_groups + c) for c in range(col_groups)]
            got = lax.ppermute(send, ("tm", "col"), pairs)
            x_in = jnp.where(tm_pos == k + 1, got, x_in)
            e_in = jnp.where(tm_pos == last - k - 1, got, e_in)
    else:
        def stage(_, carry):
            x, e = carry
            return passed_along(forward(x)[-1], "tm", 1), passed_along(backward(e)[-1], "tm", -1)

        x_in, e_in = lax.fori_loop(0, time_groups - 1, stage, (x_in, e_in))
    xs = forward(x_in)
    es = backward(e_in)
    mine = jnp.stack([jnp.stack(xs), jnp.stack([es[step_count - 2 - k] if k < step_count - 1 else e_in for k in range(step_count)])])
    mine = mine.reshape(2, step_count, own_rows, col_groups, cols).transpose(3, 0, 1, 2, 4)
    got = lax.all_to_all(mine, "col", split_axis=0, concat_axis=0, tiled=True)
    got = got.transpose(1, 2, 0, 3, 4).reshape(2, step_count, rows, cols)
    filtered = got[0]
    return filtered, filtered + got[1]


def solution(mesh):
    return jax.shard_map(
        local,
        mesh=mesh,
        in_specs=(P("tm", None, "col"), P("col"), P("tm", "col"), P("tm", None, "col"), P()),
        out_specs=(P("tm", None, "col"), P("tm", None, "col")),
        check_vma=False,
    )
```

```python
import jax
import jax.numpy as jnp
from jax import lax
from jax.sharding import PartitionSpec as P


def bf16_part(value):
    return lax.reduce_precision(value, exponent_bits=8, mantissa_bits=7)


def split_dot(state, weights, transposed):
    high = bf16_part(state)
    low = state - high
    both = jnp.concatenate([high, low], axis=0).astype(jnp.bfloat16)
    contract = 1 if transposed else 0
    prod = lax.dot_general(
        both, weights, (((1,), (contract,)), ((), ())), preferred_element_type=jnp.float32
    )
    rows = state.shape[0]
    return prod[:rows] + prod[rows:]


def three_pieces(value):
    high = bf16_part(value)
    rest = value - high
    mid = bf16_part(rest)
    return jnp.stack([high, mid, rest - mid]).astype(jnp.bfloat16)


def passed_along(shard, axis, by):
    length = lax.axis_size(axis)
    pairs = [(i, i + by) for i in range(length) if 0 <= i + by < length]
    return lax.ppermute(shard, axis, pairs)


def local(observed, input_gain, persist, coupling, pattern):
    step_count, rows, cols = observed.shape
    state_width = coupling.shape[1]
    block_count = pattern.shape[0]
    block_size = state_width // block_count
    time_groups = lax.axis_size("tm")
    col_groups = lax.axis_size("col")
    own_rows = rows // col_groups
    tm_pos = lax.axis_index("tm")

    small = jnp.concatenate([persist, input_gain[None]], axis=0)
    small_rows = 3 * (step_count + 1)
    small_pad = -small_rows % 16
    small_pieces = jnp.pad(three_pieces(small).reshape(small_rows, cols), ((0, small_pad), (0, 0)))
    coupling_rows = coupling.reshape(step_count * state_width, cols)
    seen_parts = observed.reshape(step_count, col_groups, own_rows, cols).transpose(1, 0, 2, 3)
    seen_parts = seen_parts.reshape(col_groups, step_count * own_rows, cols)
    packet = jnp.concatenate(
        [
            jnp.broadcast_to(coupling_rows[None], (col_groups,) + coupling_rows.shape),
            seen_parts,
            jnp.broadcast_to(small_pieces[None], (col_groups,) + small_pieces.shape),
        ],
        axis=1,
    )
    packet = lax.all_to_all(packet, "col", split_axis=0, concat_axis=0, tiled=True)
    n_coupling = step_count * state_width
    n_seen = step_count * own_rows
    mask = jnp.broadcast_to(
        pattern.astype(jnp.bfloat16)[:, None, :, None],
        (block_count, block_size, block_count, block_size),
    ).reshape(state_width, state_width)
    weights = (
        packet[:, :n_coupling]
        .reshape(col_groups, step_count, state_width, cols)
        .transpose(1, 2, 0, 3)
        .reshape(step_count, state_width, state_width)
    ) * mask[None]
    seen = (
        packet[:, n_coupling : n_coupling + n_seen]
        .reshape(col_groups, step_count, own_rows, cols)
        .transpose(1, 2, 0, 3)
        .reshape(step_count, own_rows, state_width)
    )
    small = packet[:, n_coupling + n_seen : n_coupling + n_seen + small_rows].astype(jnp.float32)
    small = small.reshape(col_groups, 3, step_count + 1, cols)
    small = (small[:, 0] + small[:, 1] + small[:, 2]).transpose(1, 0, 2)
    small = small.reshape(step_count + 1, state_width)
    diag = small[:step_count]
    gain = small[step_count]
    driven = gain[None, None, :] * seen.astype(jnp.float32)

    def forward(x):
        out = []
        for k in range(step_count):
            x = split_dot(x, weights[k], False) + x * diag[k][None] + driven[k]
            out.append(x)
        return out

    def backward(e):
        out = []
        for k in range(step_count - 1, -1, -1):
            w = e + driven[k]
            e = split_dot(w, weights[k], True) + w * diag[k][None]
            out.append(e)
        return out

    zeros = jnp.zeros(driven.shape[1:], jnp.float32)
    x_in, e_in = zeros, zeros
    if time_groups <= 8 and time_groups % 2 == 0:
        last = time_groups - 1
        for k in range(last):
            send = lax.cond(
                tm_pos == k,
                lambda x, e: forward(x)[-1],
                lambda x, e: backward(e)[-1],
                x_in,
                e_in,
            )
            pairs = [(k * col_groups + c, (k + 1) * col_groups + c) for c in range(col_groups)]
            pairs += [((last - k) * col_groups + c, (last - k - 1) * col_groups + c) for c in range(col_groups)]
            got = lax.ppermute(send, ("tm", "col"), pairs)
            x_in = jnp.where(tm_pos == k + 1, got, x_in)
            e_in = jnp.where(tm_pos == last - k - 1, got, e_in)
    else:
        def stage(_, carry):
            x, e = carry
            return passed_along(forward(x)[-1], "tm", 1), passed_along(backward(e)[-1], "tm", -1)

        x_in, e_in = lax.fori_loop(0, time_groups - 1, stage, (x_in, e_in))
    xs = forward(x_in)
    es = backward(e_in)
    mine = jnp.stack([jnp.stack(xs), jnp.stack([es[step_count - 2 - k] if k < step_count - 1 else e_in for k in range(step_count)])])
    mine = mine.reshape(2, step_count, own_rows, col_groups, cols).transpose(3, 0, 1, 2, 4)
    got = lax.all_to_all(mine, "col", split_axis=0, concat_axis=0, tiled=True)
    got = got.transpose(1, 2, 0, 3, 4).reshape(2, step_count, rows, cols)
    filtered = got[0]
    return filtered, filtered + got[1]


def solution(mesh):
    return jax.shard_map(
        local,
        mesh=mesh,
        in_specs=(P("tm", None, "col"), P("col"), P("tm", "col"), P("tm", None, "col"), P()),
        out_specs=(P("tm", None, "col"), P("tm", None, "col")),
        check_vma=False,
    )
```

```python
import jax
import jax.numpy as jnp
from jax import lax
from jax.sharding import PartitionSpec as P


def bf16_part(value):
    return lax.reduce_precision(value, exponent_bits=8, mantissa_bits=7)


def split_dot(state, weights, transposed):
    high = bf16_part(state)
    low = state - high
    both = jnp.concatenate([high, low], axis=0).astype(jnp.bfloat16)
    contract = 1 if transposed else 0
    prod = lax.dot_general(
        both, weights, (((1,), (contract,)), ((), ())), preferred_element_type=jnp.float32
    )
    rows = state.shape[0]
    return prod[:rows] + prod[rows:]


def three_pieces(value):
    high = bf16_part(value)
    rest = value - high
    mid = bf16_part(rest)
    return jnp.stack([high, mid, rest - mid]).astype(jnp.bfloat16)


def passed_along(shard, axis, by):
    length = lax.axis_size(axis)
    pairs = [(i, i + by) for i in range(length) if 0 <= i + by < length]
    return lax.ppermute(shard, axis, pairs)


def local(observed, input_gain, persist, coupling, pattern):
    step_count, rows, cols = observed.shape
    state_width = coupling.shape[1]
    block_count = pattern.shape[0]
    block_size = state_width // block_count
    time_groups = lax.axis_size("tm")
    col_groups = lax.axis_size("col")
    own_rows = rows // col_groups
    tm_pos = lax.axis_index("tm")

    small = jnp.concatenate([persist, input_gain[None]], axis=0)
    small_rows = 3 * (step_count + 1)
    small_pad = -small_rows % 16
    small_pieces = jnp.pad(three_pieces(small).reshape(small_rows, cols), ((0, small_pad), (0, 0)))
    coupling_rows = coupling.reshape(step_count * state_width, cols)
    seen_parts = observed.reshape(step_count, col_groups, own_rows, cols).transpose(1, 0, 2, 3)
    seen_parts = seen_parts.reshape(col_groups, step_count * own_rows, cols)
    packet = jnp.concatenate(
        [
            jnp.broadcast_to(coupling_rows[None], (col_groups,) + coupling_rows.shape),
            seen_parts,
            jnp.broadcast_to(small_pieces[None], (col_groups,) + small_pieces.shape),
        ],
        axis=1,
    )
    packet = lax.all_to_all(packet, "col", split_axis=0, concat_axis=0, tiled=True)
    n_coupling = step_count * state_width
    n_seen = step_count * own_rows
    mask = jnp.broadcast_to(
        pattern.astype(jnp.bfloat16)[:, None, :, None],
        (block_count, block_size, block_count, block_size),
    ).reshape(state_width, state_width)
    weights = (
        packet[:, :n_coupling]
        .reshape(col_groups, step_count, state_width, cols)
        .transpose(1, 2, 0, 3)
        .reshape(step_count, state_width, state_width)
    ) * mask[None]
    seen = (
        packet[:, n_coupling : n_coupling + n_seen]
        .reshape(col_groups, step_count, own_rows, cols)
        .transpose(1, 2, 0, 3)
        .reshape(step_count, own_rows, state_width)
    )
    small = packet[:, n_coupling + n_seen : n_coupling + n_seen + small_rows].astype(jnp.float32)
    small = small.reshape(col_groups, 3, step_count + 1, cols)
    small = (small[:, 0] + small[:, 1] + small[:, 2]).transpose(1, 0, 2)
    small = small.reshape(step_count + 1, state_width)
    diag = small[:step_count]
    gain = small[step_count]
    driven = gain[None, None, :] * seen.astype(jnp.float32)

    def forward(x):
        out = []
        for k in range(step_count):
            x = split_dot(x, weights[k], False) + x * diag[k][None] + driven[k]
            out.append(x)
        return out

    def backward(e):
        out = []
        for k in range(step_count - 1, -1, -1):
            w = e + driven[k]
            e = split_dot(w, weights[k], True) + w * diag[k][None]
            out.append(e)
        return out

    zeros = jnp.zeros(driven.shape[1:], jnp.float32)
    x_in, e_in = zeros, zeros
    if time_groups <= 8 and time_groups % 2 == 0:
        last = time_groups - 1
        kept_x = jnp.zeros(driven.shape, jnp.float32)
        kept_e = kept_x
        for k in range(time_groups):
            outs = lax.cond(
                tm_pos == k,
                lambda x, e: jnp.stack(forward(x)),
                lambda x, e: jnp.stack(backward(e)),
                x_in,
                e_in,
            )
            kept_x = jnp.where(tm_pos == k, outs, kept_x)
            kept_e = jnp.where(tm_pos == last - k, outs, kept_e)
            if k < last:
                pairs = [(k * col_groups + c, (k + 1) * col_groups + c) for c in range(col_groups)]
                pairs += [
                    ((last - k) * col_groups + c, (last - k - 1) * col_groups + c)
                    for c in range(col_groups)
                ]
                got = lax.ppermute(outs[-1], ("tm", "col"), pairs)
                x_in = jnp.where(tm_pos == k + 1, got, x_in)
                e_in = jnp.where(tm_pos == last - k - 1, got, e_in)
        xs = [kept_x[k] for k in range(step_count)]
        es = [kept_e[k] for k in range(step_count)]
    else:
        def stage(_, carry):
            x, e = carry
            return passed_along(forward(x)[-1], "tm", 1), passed_along(backward(e)[-1], "tm", -1)

        x_in, e_in = lax.fori_loop(0, time_groups - 1, stage, (x_in, e_in))
        xs = forward(x_in)
        es = backward(e_in)
    filtered = jnp.stack(xs)
    correction = jnp.stack([es[step_count - 2 - k] for k in range(step_count - 1)] + [e_in])
    mine = jnp.stack([filtered, filtered + correction])
    mine = mine.reshape(2, step_count, own_rows, col_groups, cols).transpose(3, 0, 1, 2, 4)
    got = lax.all_to_all(mine, "col", split_axis=0, concat_axis=0, tiled=True)
    got = got.transpose(1, 2, 0, 3, 4).reshape(2, step_count, rows, cols)
    return got[0], got[1]


def solution(mesh):
    return jax.shard_map(
        local,
        mesh=mesh,
        in_specs=(P("tm", None, "col"), P("col"), P("tm", "col"), P("tm", None, "col"), P()),
        out_specs=(P("tm", None, "col"), P("tm", None, "col")),
        check_vma=False,
    )
```

```python
import jax
import jax.numpy as jnp
from jax import lax
from jax.sharding import PartitionSpec as P


def bf16_part(value):
    return lax.reduce_precision(value, exponent_bits=8, mantissa_bits=7)


def split_dot(state, weights, transposed):
    high = bf16_part(state)
    low = state - high
    both = jnp.concatenate([high, low], axis=0).astype(jnp.bfloat16)
    contract = 1 if transposed else 0
    prod = lax.dot_general(
        both, weights, (((1,), (contract,)), ((), ())), preferred_element_type=jnp.float32
    )
    rows = state.shape[0]
    return prod[:rows] + prod[rows:]


def three_pieces(value):
    high = bf16_part(value)
    rest = value - high
    mid = bf16_part(rest)
    return jnp.stack([high, mid, rest - mid]).astype(jnp.bfloat16)


def passed_along(shard, axis, by):
    length = lax.axis_size(axis)
    pairs = [(i, i + by) for i in range(length) if 0 <= i + by < length]
    return lax.ppermute(shard, axis, pairs)


def local(observed, input_gain, persist, coupling, pattern):
    step_count, rows, cols = observed.shape
    state_width = coupling.shape[1]
    block_count = pattern.shape[0]
    block_size = state_width // block_count
    time_groups = lax.axis_size("tm")
    col_groups = lax.axis_size("col")
    own_rows = rows // col_groups
    tm_pos = lax.axis_index("tm")

    col_pos = lax.axis_index("col")
    small = jnp.concatenate([persist, input_gain[None]], axis=0)
    small_rows = 3 * (step_count + 1)
    small_pad = -small_rows % 16
    small_pieces = jnp.pad(three_pieces(small).reshape(small_rows, cols), ((0, small_pad), (0, 0)))
    coupling_rows = coupling.reshape(step_count * state_width, cols)
    seen_parts = observed.reshape(step_count, col_groups, own_rows, cols).transpose(1, 0, 2, 3)
    seen_parts = seen_parts.reshape(col_groups, step_count * own_rows, cols)
    chunks = []
    for shift in range(col_groups):
        dest = (col_pos + shift) % col_groups
        seen_d = lax.dynamic_index_in_dim(seen_parts, dest, 0, keepdims=False)
        chunk = jnp.concatenate([coupling_rows, seen_d, small_pieces], axis=0)
        if shift:
            pairs = [
                (t * col_groups + c, t * col_groups + (c + shift) % col_groups)
                for t in range(time_groups)
                for c in range(col_groups)
            ]
            chunk = lax.ppermute(chunk, ("tm", "col"), pairs)
        chunks.append(chunk)
    by_shift = jnp.stack(chunks[::-1] + chunks[::-1])
    packet = lax.dynamic_slice_in_dim(by_shift, col_groups - 1 - col_pos, col_groups, 0)
    n_coupling = step_count * state_width
    n_seen = step_count * own_rows
    mask = jnp.broadcast_to(
        pattern.astype(jnp.bfloat16)[:, None, :, None],
        (block_count, block_size, block_count, block_size),
    ).reshape(state_width, state_width)
    weights = (
        packet[:, :n_coupling]
        .reshape(col_groups, step_count, state_width, cols)
        .transpose(1, 2, 0, 3)
        .reshape(step_count, state_width, state_width)
    ) * mask[None]
    seen = (
        packet[:, n_coupling : n_coupling + n_seen]
        .reshape(col_groups, step_count, own_rows, cols)
        .transpose(1, 2, 0, 3)
        .reshape(step_count, own_rows, state_width)
    )
    small = packet[:, n_coupling + n_seen : n_coupling + n_seen + small_rows].astype(jnp.float32)
    small = small.reshape(col_groups, 3, step_count + 1, cols)
    small = (small[:, 0] + small[:, 1] + small[:, 2]).transpose(1, 0, 2)
    small = small.reshape(step_count + 1, state_width)
    diag = small[:step_count]
    gain = small[step_count]
    driven = gain[None, None, :] * seen.astype(jnp.float32)

    def forward(x):
        out = []
        for k in range(step_count):
            x = split_dot(x, weights[k], False) + x * diag[k][None] + driven[k]
            out.append(x)
        return out

    def backward(e):
        out = []
        for k in range(step_count - 1, -1, -1):
            w = e + driven[k]
            e = split_dot(w, weights[k], True) + w * diag[k][None]
            out.append(e)
        return out

    zeros = jnp.zeros(driven.shape[1:], jnp.float32)
    x_in, e_in = zeros, zeros
    if time_groups <= 8 and time_groups % 2 == 0:
        last = time_groups - 1
        for k in range(last):
            send = lax.cond(
                tm_pos == k,
                lambda x, e: forward(x)[-1],
                lambda x, e: backward(e)[-1],
                x_in,
                e_in,
            )
            pairs = [(k * col_groups + c, (k + 1) * col_groups + c) for c in range(col_groups)]
            pairs += [((last - k) * col_groups + c, (last - k - 1) * col_groups + c) for c in range(col_groups)]
            got = lax.ppermute(send, ("tm", "col"), pairs)
            x_in = jnp.where(tm_pos == k + 1, got, x_in)
            e_in = jnp.where(tm_pos == last - k - 1, got, e_in)
    else:
        def stage(_, carry):
            x, e = carry
            return passed_along(forward(x)[-1], "tm", 1), passed_along(backward(e)[-1], "tm", -1)

        x_in, e_in = lax.fori_loop(0, time_groups - 1, stage, (x_in, e_in))
    xs = forward(x_in)
    es = backward(e_in)
    mine = jnp.stack([jnp.stack(xs), jnp.stack([es[step_count - 2 - k] if k < step_count - 1 else e_in for k in range(step_count)])])
    mine = mine.reshape(2, step_count, own_rows, col_groups, cols).transpose(3, 0, 1, 2, 4)
    got = lax.all_to_all(mine, "col", split_axis=0, concat_axis=0, tiled=True)
    got = got.transpose(1, 2, 0, 3, 4).reshape(2, step_count, rows, cols)
    filtered = got[0]
    return filtered, filtered + got[1]


def solution(mesh):
    return jax.shard_map(
        local,
        mesh=mesh,
        in_specs=(P("tm", None, "col"), P("col"), P("tm", "col"), P("tm", None, "col"), P()),
        out_specs=(P("tm", None, "col"), P("tm", None, "col")),
        check_vma=False,
    )
```

```python
import jax
import jax.numpy as jnp
from jax import lax
from jax.sharding import PartitionSpec as P


def bf16_part(value):
    return lax.reduce_precision(value, exponent_bits=8, mantissa_bits=7)


def split_dot(state, weights, transposed):
    high = bf16_part(state)
    low = state - high
    both = jnp.concatenate([high, low], axis=0).astype(jnp.bfloat16)
    contract = 1 if transposed else 0
    prod = lax.dot_general(
        both, weights, (((1,), (contract,)), ((), ())), preferred_element_type=jnp.float32
    )
    rows = state.shape[0]
    return prod[:rows] + prod[rows:]


def three_pieces(value):
    high = bf16_part(value)
    rest = value - high
    mid = bf16_part(rest)
    return jnp.stack([high, mid, rest - mid]).astype(jnp.bfloat16)


def passed_along(shard, axis, by):
    length = lax.axis_size(axis)
    pairs = [(i, i + by) for i in range(length) if 0 <= i + by < length]
    return lax.ppermute(shard, axis, pairs)


def local(observed, input_gain, persist, coupling, pattern):
    step_count, rows, cols = observed.shape
    state_width = coupling.shape[1]
    block_count = pattern.shape[0]
    block_size = state_width // block_count
    time_groups = lax.axis_size("tm")
    col_groups = lax.axis_size("col")
    own_rows = rows // col_groups
    tm_pos = lax.axis_index("tm")

    col_pos = lax.axis_index("col")
    small = jnp.concatenate([persist, input_gain[None]], axis=0)
    small_rows = 3 * (step_count + 1)
    small_pad = -small_rows % 16
    small_pieces = jnp.pad(three_pieces(small).reshape(small_rows, cols), ((0, small_pad), (0, 0)))
    coupling_rows = coupling.reshape(step_count * state_width, cols)
    seen_parts = observed.reshape(step_count, col_groups, own_rows, cols).transpose(1, 0, 2, 3)
    seen_parts = seen_parts.reshape(col_groups, step_count * own_rows, cols)
    chunks = []
    for shift in range(col_groups):
        dest = (col_pos + shift) % col_groups
        seen_d = lax.dynamic_index_in_dim(seen_parts, dest, 0, keepdims=False)
        chunk = jnp.concatenate([coupling_rows, seen_d, small_pieces], axis=0)
        if shift:
            pairs = [
                (t * col_groups + c, t * col_groups + (c + shift) % col_groups)
                for t in range(time_groups)
                for c in range(col_groups)
            ]
            chunk = lax.ppermute(chunk, ("tm", "col"), pairs)
        chunks.append(chunk)
    def from_source(j):
        which = (col_pos - j) % col_groups
        out = chunks[0]
        for shift in range(1, col_groups):
            out = jnp.where(which == shift, chunks[shift], out)
        return out

    packet = jnp.stack([from_source(j) for j in range(col_groups)])
    n_coupling = step_count * state_width
    n_seen = step_count * own_rows
    mask = jnp.broadcast_to(
        pattern.astype(jnp.bfloat16)[:, None, :, None],
        (block_count, block_size, block_count, block_size),
    ).reshape(state_width, state_width)
    weights = (
        packet[:, :n_coupling]
        .reshape(col_groups, step_count, state_width, cols)
        .transpose(1, 2, 0, 3)
        .reshape(step_count, state_width, state_width)
    ) * mask[None]
    seen = (
        packet[:, n_coupling : n_coupling + n_seen]
        .reshape(col_groups, step_count, own_rows, cols)
        .transpose(1, 2, 0, 3)
        .reshape(step_count, own_rows, state_width)
    )
    small = packet[:, n_coupling + n_seen : n_coupling + n_seen + small_rows].astype(jnp.float32)
    small = small.reshape(col_groups, 3, step_count + 1, cols)
    small = (small[:, 0] + small[:, 1] + small[:, 2]).transpose(1, 0, 2)
    small = small.reshape(step_count + 1, state_width)
    diag = small[:step_count]
    gain = small[step_count]
    driven = gain[None, None, :] * seen.astype(jnp.float32)

    def forward(x):
        out = []
        for k in range(step_count):
            x = split_dot(x, weights[k], False) + x * diag[k][None] + driven[k]
            out.append(x)
        return out

    def backward(e):
        out = []
        for k in range(step_count - 1, -1, -1):
            w = e + driven[k]
            e = split_dot(w, weights[k], True) + w * diag[k][None]
            out.append(e)
        return out

    zeros = jnp.zeros(driven.shape[1:], jnp.float32)
    x_in, e_in = zeros, zeros
    if time_groups <= 8 and time_groups % 2 == 0:
        last = time_groups - 1
        for k in range(last):
            send = lax.cond(
                tm_pos == k,
                lambda x, e: forward(x)[-1],
                lambda x, e: backward(e)[-1],
                x_in,
                e_in,
            )
            pairs = [(k * col_groups + c, (k + 1) * col_groups + c) for c in range(col_groups)]
            pairs += [((last - k) * col_groups + c, (last - k - 1) * col_groups + c) for c in range(col_groups)]
            got = lax.ppermute(send, ("tm", "col"), pairs)
            x_in = jnp.where(tm_pos == k + 1, got, x_in)
            e_in = jnp.where(tm_pos == last - k - 1, got, e_in)
    else:
        def stage(_, carry):
            x, e = carry
            return passed_along(forward(x)[-1], "tm", 1), passed_along(backward(e)[-1], "tm", -1)

        x_in, e_in = lax.fori_loop(0, time_groups - 1, stage, (x_in, e_in))
    xs = forward(x_in)
    es = backward(e_in)
    mine = jnp.stack([jnp.stack(xs), jnp.stack([es[step_count - 2 - k] if k < step_count - 1 else e_in for k in range(step_count)])])
    mine = mine.reshape(2, step_count, own_rows, col_groups, cols).transpose(3, 0, 1, 2, 4)
    got = lax.all_to_all(mine, "col", split_axis=0, concat_axis=0, tiled=True)
    got = got.transpose(1, 2, 0, 3, 4).reshape(2, step_count, rows, cols)
    filtered = got[0]
    return filtered, filtered + got[1]


def solution(mesh):
    return jax.shard_map(
        local,
        mesh=mesh,
        in_specs=(P("tm", None, "col"), P("col"), P("tm", "col"), P("tm", None, "col"), P()),
        out_specs=(P("tm", None, "col"), P("tm", None, "col")),
        check_vma=False,
    )
```

```python
import jax
import jax.numpy as jnp
from jax import lax
from jax.sharding import PartitionSpec as P


def bf16_part(value):
    return lax.reduce_precision(value, exponent_bits=8, mantissa_bits=7)


def split_dot(state, weights, transposed):
    high = bf16_part(state)
    low = state - high
    both = jnp.concatenate([high, low], axis=0).astype(jnp.bfloat16)
    contract = 1 if transposed else 0
    prod = lax.dot_general(
        both, weights, (((1,), (contract,)), ((), ())), preferred_element_type=jnp.float32
    )
    rows = state.shape[0]
    return prod[:rows] + prod[rows:]


def three_pieces(value):
    high = bf16_part(value)
    rest = value - high
    mid = bf16_part(rest)
    return jnp.stack([high, mid, rest - mid]).astype(jnp.bfloat16)


def passed_along(shard, axis, by):
    length = lax.axis_size(axis)
    pairs = [(i, i + by) for i in range(length) if 0 <= i + by < length]
    return lax.ppermute(shard, axis, pairs)


def local(observed, input_gain, persist, coupling, pattern):
    step_count, rows, cols = observed.shape
    state_width = coupling.shape[1]
    block_count = pattern.shape[0]
    block_size = state_width // block_count
    time_groups = lax.axis_size("tm")
    col_groups = lax.axis_size("col")
    own_rows = rows // col_groups
    tm_pos = lax.axis_index("tm")

    col_pos = lax.axis_index("col")
    small = jnp.concatenate([persist, input_gain[None]], axis=0)
    small_rows = 3 * (step_count + 1)
    small_pad = -small_rows % 16
    small_pieces = jnp.pad(three_pieces(small).reshape(small_rows, cols), ((0, small_pad), (0, 0)))
    coupling_rows = coupling.reshape(step_count * state_width, cols)
    seen_parts = observed.reshape(step_count, col_groups, own_rows, cols).transpose(1, 0, 2, 3)
    seen_parts = seen_parts.reshape(col_groups, step_count * own_rows, cols)
    chunks = []
    for shift in range(col_groups):
        dest = (col_pos + shift) % col_groups
        seen_d = lax.dynamic_index_in_dim(seen_parts, dest, 0, keepdims=False)
        chunk = jnp.concatenate([coupling_rows, seen_d, small_pieces], axis=0)
        if shift:
            pairs = [
                (t * col_groups + c, t * col_groups + (c + shift) % col_groups)
                for t in range(time_groups)
                for c in range(col_groups)
            ]
            chunk = lax.ppermute(chunk, ("tm", "col"), pairs)
        chunks.append(chunk)
    def from_source(j):
        which = (col_pos - j) % col_groups
        out = chunks[0]
        for shift in range(1, col_groups):
            out = jnp.where(which == shift, chunks[shift], out)
        return out

    packet = jnp.stack([from_source(j) for j in range(col_groups)])
    n_coupling = step_count * state_width
    n_seen = step_count * own_rows
    mask = jnp.broadcast_to(
        pattern.astype(jnp.bfloat16)[:, None, :, None],
        (block_count, block_size, block_count, block_size),
    ).reshape(state_width, state_width)
    weights = (
        packet[:, :n_coupling]
        .reshape(col_groups, step_count, state_width, cols)
        .transpose(1, 2, 0, 3)
        .reshape(step_count, state_width, state_width)
    ) * mask[None]
    seen = (
        packet[:, n_coupling : n_coupling + n_seen]
        .reshape(col_groups, step_count, own_rows, cols)
        .transpose(1, 2, 0, 3)
        .reshape(step_count, own_rows, state_width)
    )
    small = packet[:, n_coupling + n_seen : n_coupling + n_seen + small_rows].astype(jnp.float32)
    small = small.reshape(col_groups, 3, step_count + 1, cols)
    small = (small[:, 0] + small[:, 1] + small[:, 2]).transpose(1, 0, 2)
    small = small.reshape(step_count + 1, state_width)
    diag = small[:step_count]
    gain = small[step_count]
    driven = gain[None, None, :] * seen.astype(jnp.float32)

    def forward(x):
        out = []
        for k in range(step_count):
            x = split_dot(x, weights[k], False) + x * diag[k][None] + driven[k]
            out.append(x)
        return out

    def backward(e):
        out = []
        for k in range(step_count - 1, -1, -1):
            w = e + driven[k]
            e = split_dot(w, weights[k], True) + w * diag[k][None]
            out.append(e)
        return out

    zeros = jnp.zeros(driven.shape[1:], jnp.float32)
    x_in, e_in = zeros, zeros
    if time_groups <= 8 and time_groups % 2 == 0:
        last = time_groups - 1
        for k in range(last):
            send = lax.cond(
                tm_pos == k,
                lambda x, e: forward(x)[-1],
                lambda x, e: backward(e)[-1],
                x_in,
                e_in,
            )
            pairs = [(k * col_groups + c, (k + 1) * col_groups + c) for c in range(col_groups)]
            pairs += [((last - k) * col_groups + c, (last - k - 1) * col_groups + c) for c in range(col_groups)]
            got = lax.ppermute(send, ("tm", "col"), pairs)
            x_in = jnp.where(tm_pos == k + 1, got, x_in)
            e_in = jnp.where(tm_pos == last - k - 1, got, e_in)
    else:
        def stage(_, carry):
            x, e = carry
            return passed_along(forward(x)[-1], "tm", 1), passed_along(backward(e)[-1], "tm", -1)

        x_in, e_in = lax.fori_loop(0, time_groups - 1, stage, (x_in, e_in))
    xs = forward(x_in)
    es = backward(e_in)
    filtered = jnp.stack(xs)
    correction = jnp.stack([es[step_count - 2 - k] for k in range(step_count - 1)] + [e_in])
    mine = jnp.stack([filtered, filtered + correction])
    parts = [mine[:, :, :, j * cols : (j + 1) * cols] for j in range(col_groups)]

    def pick(options, which):
        out = options[0]
        for j in range(1, col_groups):
            out = jnp.where(which == j, options[j], out)
        return out

    arrived = []
    for shift in range(col_groups):
        piece = pick(parts, (col_pos + shift) % col_groups)
        if shift:
            pairs = [
                (t * col_groups + c, t * col_groups + (c + shift) % col_groups)
                for t in range(time_groups)
                for c in range(col_groups)
            ]
            piece = lax.ppermute(piece, ("tm", "col"), pairs)
        arrived.append(piece)
    got = jnp.stack([pick(arrived, (col_pos - j) % col_groups) for j in range(col_groups)], axis=2)
    got = got.reshape(2, step_count, rows, cols)
    return got[0], got[1]


def solution(mesh):
    return jax.shard_map(
        local,
        mesh=mesh,
        in_specs=(P("tm", None, "col"), P("col"), P("tm", "col"), P("tm", None, "col"), P()),
        out_specs=(P("tm", None, "col"), P("tm", None, "col")),
        check_vma=False,
    )
```

```python
import jax
import jax.numpy as jnp
from jax import lax
from jax.sharding import PartitionSpec as P


def bf16_part(value):
    return lax.reduce_precision(value, exponent_bits=8, mantissa_bits=7)


def split_dot(state, weights, transposed):
    high = bf16_part(state)
    low = state - high
    both = jnp.concatenate([high, low], axis=0).astype(jnp.bfloat16)
    contract = 1 if transposed else 0
    prod = lax.dot_general(
        both, weights, (((1,), (contract,)), ((), ())), preferred_element_type=jnp.float32
    )
    rows = state.shape[0]
    return prod[:rows] + prod[rows:]


def three_pieces(value):
    high = bf16_part(value)
    rest = value - high
    mid = bf16_part(rest)
    return jnp.stack([high, mid, rest - mid]).astype(jnp.bfloat16)


def passed_along(shard, axis, by):
    length = lax.axis_size(axis)
    pairs = [(i, i + by) for i in range(length) if 0 <= i + by < length]
    return lax.ppermute(shard, axis, pairs)


def local(observed, input_gain, persist, coupling, pattern):
    step_count, rows, cols = observed.shape
    state_width = coupling.shape[1]
    block_count = pattern.shape[0]
    block_size = state_width // block_count
    time_groups = lax.axis_size("tm")
    col_groups = lax.axis_size("col")
    own_rows = rows // col_groups
    tm_pos = lax.axis_index("tm")

    col_pos = lax.axis_index("col")
    small = jnp.concatenate([persist, input_gain[None]], axis=0)
    small_rows = 3 * (step_count + 1)
    small_pad = -small_rows % 16
    small_pieces = jnp.pad(three_pieces(small).reshape(small_rows, cols), ((0, small_pad), (0, 0)))
    coupling_rows = coupling.reshape(step_count * state_width, cols)
    seen_parts = observed.reshape(step_count, col_groups, own_rows, cols).transpose(1, 0, 2, 3)
    seen_parts = seen_parts.reshape(col_groups, step_count * own_rows, cols)
    chunks = []
    for shift in range(col_groups):
        dest = (col_pos + shift) % col_groups
        seen_d = lax.dynamic_index_in_dim(seen_parts, dest, 0, keepdims=False)
        chunk = jnp.concatenate([coupling_rows, seen_d, small_pieces], axis=0)
        if shift:
            pairs = [
                (t * col_groups + c, t * col_groups + (c + shift) % col_groups)
                for t in range(time_groups)
                for c in range(col_groups)
            ]
            chunk = lax.ppermute(chunk, ("tm", "col"), pairs)
        chunks.append(chunk)
    def from_source(j):
        which = (col_pos - j) % col_groups
        out = chunks[0]
        for shift in range(1, col_groups):
            out = jnp.where(which == shift, chunks[shift], out)
        return out

    packet = jnp.stack([from_source(j) for j in range(col_groups)])
    n_coupling = step_count * state_width
    n_seen = step_count * own_rows
    mask = jnp.broadcast_to(
        pattern.astype(jnp.bfloat16)[:, None, :, None],
        (block_count, block_size, block_count, block_size),
    ).reshape(state_width, state_width)
    weights = (
        packet[:, :n_coupling]
        .reshape(col_groups, step_count, state_width, cols)
        .transpose(1, 2, 0, 3)
        .reshape(step_count, state_width, state_width)
    ) * mask[None]
    seen = (
        packet[:, n_coupling : n_coupling + n_seen]
        .reshape(col_groups, step_count, own_rows, cols)
        .transpose(1, 2, 0, 3)
        .reshape(step_count, own_rows, state_width)
    )
    small = packet[:, n_coupling + n_seen : n_coupling + n_seen + small_rows].astype(jnp.float32)
    small = small.reshape(col_groups, 3, step_count + 1, cols)
    small = (small[:, 0] + small[:, 1] + small[:, 2]).transpose(1, 0, 2)
    small = small.reshape(step_count + 1, state_width)
    diag = small[:step_count]
    gain = small[step_count]
    driven = gain[None, None, :] * seen.astype(jnp.float32)

    def forward(x):
        out = []
        for k in range(step_count):
            x = split_dot(x, weights[k], False) + x * diag[k][None] + driven[k]
            out.append(x)
        return out

    def backward(e):
        out = []
        for k in range(step_count - 1, -1, -1):
            w = e + driven[k]
            e = split_dot(w, weights[k], True) + w * diag[k][None]
            out.append(e)
        return out

    zeros = jnp.zeros(driven.shape[1:], jnp.float32)
    x_in, e_in = zeros, zeros
    if time_groups <= 8 and time_groups % 2 == 0:
        last = time_groups - 1
        for k in range(last):
            send = lax.cond(
                tm_pos == k,
                lambda x, e: forward(x)[-1],
                lambda x, e: backward(e)[-1],
                x_in,
                e_in,
            )
            pairs = [(k * col_groups + c, (k + 1) * col_groups + c) for c in range(col_groups)]
            pairs += [((last - k) * col_groups + c, (last - k - 1) * col_groups + c) for c in range(col_groups)]
            got = lax.ppermute(send, ("tm", "col"), pairs)
            x_in = jnp.where(tm_pos == k + 1, got, x_in)
            e_in = jnp.where(tm_pos == last - k - 1, got, e_in)
    else:
        def stage(_, carry):
            x, e = carry
            return passed_along(forward(x)[-1], "tm", 1), passed_along(backward(e)[-1], "tm", -1)

        x_in, e_in = lax.fori_loop(0, time_groups - 1, stage, (x_in, e_in))
    xs = forward(x_in)
    es = backward(e_in)
    filtered = jnp.stack(xs)
    correction = jnp.stack([es[step_count - 2 - k] for k in range(step_count - 1)] + [e_in])
    mine = jnp.stack([filtered, filtered + correction])
    parts = [mine[:, :, :, j * cols : (j + 1) * cols] for j in range(col_groups)]

    def pick(options, which):
        out = options[0]
        for j in range(1, col_groups):
            out = jnp.where(which == j, options[j], out)
        return out

    arrived = []
    for shift in range(col_groups):
        piece = pick(parts, (col_pos + shift) % col_groups)
        if shift:
            pairs = [
                (t * col_groups + c, t * col_groups + (c + shift) % col_groups)
                for t in range(time_groups)
                for c in range(col_groups)
            ]
            piece = lax.ppermute(piece, ("tm", "col"), pairs)
        arrived.append(piece)
    outputs = []
    for kind in range(2):
        mine_kind = [piece[kind] for piece in arrived]
        outputs.append(
            jnp.concatenate([pick(mine_kind, (col_pos - j) % col_groups) for j in range(col_groups)], axis=1)
        )
    return outputs[0], outputs[1]


def solution(mesh):
    return jax.shard_map(
        local,
        mesh=mesh,
        in_specs=(P("tm", None, "col"), P("col"), P("tm", "col"), P("tm", None, "col"), P()),
        out_specs=(P("tm", None, "col"), P("tm", None, "col")),
        check_vma=False,
    )
```

```python
import jax
import jax.numpy as jnp
from jax import lax
from jax.sharding import PartitionSpec as P
from jax.experimental import pallas as pl
from jax.experimental.pallas import tpu as pltpu


def bf16_part(value):
    return lax.reduce_precision(value, exponent_bits=8, mantissa_bits=7)


def split_dot(state, weights, transposed):
    high = bf16_part(state)
    low = state - high
    both = jnp.concatenate([high, low], axis=0).astype(jnp.bfloat16)
    contract = 1 if transposed else 0
    prod = lax.dot_general(
        both, weights, (((1,), (contract,)), ((), ())), preferred_element_type=jnp.float32
    )
    rows = state.shape[0]
    return prod[:rows] + prod[rows:]


def three_pieces(value):
    high = bf16_part(value)
    rest = value - high
    mid = bf16_part(rest)
    return jnp.stack([high, mid, rest - mid]).astype(jnp.bfloat16)


def stage_kernel(flag_ref, x_ref, e_ref, w_ref, diag_ref, drive_ref, out_ref):
    step_count = w_ref.shape[0]

    def halves(value):
        high = value.astype(jnp.bfloat16)
        low = (value - high.astype(jnp.float32)).astype(jnp.bfloat16)
        return high, low

    @pl.when(flag_ref[0] == 1)
    def _():
        x = x_ref[...]
        for k in range(step_count):
            high, low = halves(x)
            w = w_ref[k]
            prod = jnp.dot(high, w, preferred_element_type=jnp.float32)
            prod = prod + jnp.dot(low, w, preferred_element_type=jnp.float32)
            x = prod + x * diag_ref[k : k + 1, :] + drive_ref[k]
            out_ref[k] = x

    @pl.when(flag_ref[0] != 1)
    def _():
        e = e_ref[...]
        for j, k in enumerate(range(step_count - 1, -1, -1)):
            z = e + drive_ref[k]
            high, low = halves(z)
            w = w_ref[k]
            dims = (((1,), (1,)), ((), ()))
            prod = lax.dot_general(high, w, dims, preferred_element_type=jnp.float32)
            prod = prod + lax.dot_general(low, w, dims, preferred_element_type=jnp.float32)
            e = prod + z * diag_ref[k : k + 1, :]
            out_ref[j] = e


def run_stage(flag, x, e, weights, diag, driven):
    vmem = pl.BlockSpec(memory_space=pltpu.VMEM)
    return pl.pallas_call(
        stage_kernel,
        out_shape=jax.ShapeDtypeStruct(driven.shape, jnp.float32),
        in_specs=[pl.BlockSpec(memory_space=pltpu.SMEM)] + [vmem] * 5,
        out_specs=vmem,
    )(flag, x, e, weights, diag, driven)


def passed_along(shard, axis, by):
    length = lax.axis_size(axis)
    pairs = [(i, i + by) for i in range(length) if 0 <= i + by < length]
    return lax.ppermute(shard, axis, pairs)


def local(observed, input_gain, persist, coupling, pattern):
    step_count, rows, cols = observed.shape
    state_width = coupling.shape[1]
    block_count = pattern.shape[0]
    block_size = state_width // block_count
    time_groups = lax.axis_size("tm")
    col_groups = lax.axis_size("col")
    own_rows = rows // col_groups
    tm_pos = lax.axis_index("tm")

    col_pos = lax.axis_index("col")
    small = jnp.concatenate([persist, input_gain[None]], axis=0)
    small_rows = 3 * (step_count + 1)
    small_pad = -small_rows % 16
    small_pieces = jnp.pad(three_pieces(small).reshape(small_rows, cols), ((0, small_pad), (0, 0)))
    coupling_rows = coupling.reshape(step_count * state_width, cols)
    seen_parts = observed.reshape(step_count, col_groups, own_rows, cols).transpose(1, 0, 2, 3)
    seen_parts = seen_parts.reshape(col_groups, step_count * own_rows, cols)
    chunks = []
    for shift in range(col_groups):
        dest = (col_pos + shift) % col_groups
        seen_d = lax.dynamic_index_in_dim(seen_parts, dest, 0, keepdims=False)
        chunk = jnp.concatenate([coupling_rows, seen_d, small_pieces], axis=0)
        if shift:
            pairs = [
                (t * col_groups + c, t * col_groups + (c + shift) % col_groups)
                for t in range(time_groups)
                for c in range(col_groups)
            ]
            chunk = lax.ppermute(chunk, ("tm", "col"), pairs)
        chunks.append(chunk)
    def from_source(j):
        which = (col_pos - j) % col_groups
        out = chunks[0]
        for shift in range(1, col_groups):
            out = jnp.where(which == shift, chunks[shift], out)
        return out

    packet = jnp.stack([from_source(j) for j in range(col_groups)])
    n_coupling = step_count * state_width
    n_seen = step_count * own_rows
    mask = jnp.broadcast_to(
        pattern.astype(jnp.bfloat16)[:, None, :, None],
        (block_count, block_size, block_count, block_size),
    ).reshape(state_width, state_width)
    weights = (
        packet[:, :n_coupling]
        .reshape(col_groups, step_count, state_width, cols)
        .transpose(1, 2, 0, 3)
        .reshape(step_count, state_width, state_width)
    ) * mask[None]
    seen = (
        packet[:, n_coupling : n_coupling + n_seen]
        .reshape(col_groups, step_count, own_rows, cols)
        .transpose(1, 2, 0, 3)
        .reshape(step_count, own_rows, state_width)
    )
    small = packet[:, n_coupling + n_seen : n_coupling + n_seen + small_rows].astype(jnp.float32)
    small = small.reshape(col_groups, 3, step_count + 1, cols)
    small = (small[:, 0] + small[:, 1] + small[:, 2]).transpose(1, 0, 2)
    small = small.reshape(step_count + 1, state_width)
    diag = small[:step_count]
    gain = small[step_count]
    driven = gain[None, None, :] * seen.astype(jnp.float32)

    def forward(x):
        out = []
        for k in range(step_count):
            x = split_dot(x, weights[k], False) + x * diag[k][None] + driven[k]
            out.append(x)
        return out

    def backward(e):
        out = []
        for k in range(step_count - 1, -1, -1):
            w = e + driven[k]
            e = split_dot(w, weights[k], True) + w * diag[k][None]
            out.append(e)
        return out

    zeros = jnp.zeros(driven.shape[1:], jnp.float32)
    x_in, e_in = zeros, zeros
    if time_groups <= 8 and time_groups % 2 == 0:
        last = time_groups - 1
        for k in range(last):
            flag = (tm_pos == k).astype(jnp.int32).reshape(1)
            send = run_stage(flag, x_in, e_in, weights, diag, driven)[-1]
            pairs = [(k * col_groups + c, (k + 1) * col_groups + c) for c in range(col_groups)]
            pairs += [((last - k) * col_groups + c, (last - k - 1) * col_groups + c) for c in range(col_groups)]
            got = lax.ppermute(send, ("tm", "col"), pairs)
            x_in = jnp.where(tm_pos == k + 1, got, x_in)
            e_in = jnp.where(tm_pos == last - k - 1, got, e_in)
    else:
        def stage(_, carry):
            x, e = carry
            return passed_along(forward(x)[-1], "tm", 1), passed_along(backward(e)[-1], "tm", -1)

        x_in, e_in = lax.fori_loop(0, time_groups - 1, stage, (x_in, e_in))
    xs = forward(x_in)
    es = backward(e_in)
    filtered = jnp.stack(xs)
    correction = jnp.stack([es[step_count - 2 - k] for k in range(step_count - 1)] + [e_in])
    mine = jnp.stack([filtered, filtered + correction])
    parts = [mine[:, :, :, j * cols : (j + 1) * cols] for j in range(col_groups)]

    def pick(options, which):
        out = options[0]
        for j in range(1, col_groups):
            out = jnp.where(which == j, options[j], out)
        return out

    arrived = []
    for shift in range(col_groups):
        piece = pick(parts, (col_pos + shift) % col_groups)
        if shift:
            pairs = [
                (t * col_groups + c, t * col_groups + (c + shift) % col_groups)
                for t in range(time_groups)
                for c in range(col_groups)
            ]
            piece = lax.ppermute(piece, ("tm", "col"), pairs)
        arrived.append(piece)
    outputs = []
    for kind in range(2):
        mine_kind = [piece[kind] for piece in arrived]
        outputs.append(
            jnp.concatenate([pick(mine_kind, (col_pos - j) % col_groups) for j in range(col_groups)], axis=1)
        )
    return outputs[0], outputs[1]


def solution(mesh):
    return jax.shard_map(
        local,
        mesh=mesh,
        in_specs=(P("tm", None, "col"), P("col"), P("tm", "col"), P("tm", None, "col"), P()),
        out_specs=(P("tm", None, "col"), P("tm", None, "col")),
        check_vma=False,
    )
```

```python
import jax
import jax.numpy as jnp
from jax import lax
from jax.sharding import PartitionSpec as P


def bf16_part(value):
    return lax.reduce_precision(value, exponent_bits=8, mantissa_bits=7)


def split_dot(state, weights, transposed):
    high = bf16_part(state)
    low = state - high
    both = jnp.concatenate([high, low], axis=0).astype(jnp.bfloat16)
    contract = 1 if transposed else 0
    prod = lax.dot_general(
        both, weights, (((1,), (contract,)), ((), ())), preferred_element_type=jnp.float32
    )
    rows = state.shape[0]
    return prod[:rows] + prod[rows:]


def three_pieces(value):
    high = bf16_part(value)
    rest = value - high
    mid = bf16_part(rest)
    return jnp.stack([high, mid, rest - mid]).astype(jnp.bfloat16)


def passed_along(shard, axis, by):
    length = lax.axis_size(axis)
    pairs = [(i, i + by) for i in range(length) if 0 <= i + by < length]
    return lax.ppermute(shard, axis, pairs)


def local(observed, input_gain, persist, coupling, pattern):
    step_count, rows, cols = observed.shape
    state_width = coupling.shape[1]
    block_count = pattern.shape[0]
    block_size = state_width // block_count
    time_groups = lax.axis_size("tm")
    col_groups = lax.axis_size("col")
    own_rows = rows // col_groups
    tm_pos = lax.axis_index("tm")

    col_pos = lax.axis_index("col")
    small = jnp.concatenate([persist, input_gain[None]], axis=0)
    small_rows = 3 * (step_count + 1)
    small_pad = -small_rows % 16
    small_pieces = jnp.pad(three_pieces(small).reshape(small_rows, cols), ((0, small_pad), (0, 0)))
    coupling_rows = coupling.reshape(step_count * state_width, cols)
    seen_parts = observed.reshape(step_count, col_groups, own_rows, cols).transpose(1, 0, 2, 3)
    seen_parts = seen_parts.reshape(col_groups, step_count * own_rows, cols)
    chunks = []
    for shift in range(col_groups):
        dest = (col_pos + shift) % col_groups
        seen_d = lax.dynamic_index_in_dim(seen_parts, dest, 0, keepdims=False)
        chunk = jnp.concatenate([coupling_rows, seen_d, small_pieces], axis=0)
        if shift:
            pairs = [
                (t * col_groups + c, t * col_groups + (c + shift) % col_groups)
                for t in range(time_groups)
                for c in range(col_groups)
            ]
            chunk = lax.ppermute(chunk, ("tm", "col"), pairs)
        chunks.append(chunk)
    def from_source(j):
        which = (col_pos - j) % col_groups
        out = chunks[0]
        for shift in range(1, col_groups):
            out = jnp.where(which == shift, chunks[shift], out)
        return out

    sourced = [from_source(j) for j in range(col_groups)]
    packet = jnp.stack(sourced)
    n_coupling = step_count * state_width
    n_seen = step_count * own_rows
    mask = jnp.broadcast_to(
        pattern.astype(jnp.bfloat16)[:, None, :, None],
        (block_count, block_size, block_count, block_size),
    ).reshape(state_width, state_width)
    weights = jnp.concatenate(
        [part[:n_coupling].reshape(step_count, state_width, cols) for part in sourced], axis=2
    ) * mask[None]
    seen = (
        packet[:, n_coupling : n_coupling + n_seen]
        .reshape(col_groups, step_count, own_rows, cols)
        .transpose(1, 2, 0, 3)
        .reshape(step_count, own_rows, state_width)
    )
    small = packet[:, n_coupling + n_seen : n_coupling + n_seen + small_rows].astype(jnp.float32)
    small = small.reshape(col_groups, 3, step_count + 1, cols)
    small = (small[:, 0] + small[:, 1] + small[:, 2]).transpose(1, 0, 2)
    small = small.reshape(step_count + 1, state_width)
    diag = small[:step_count]
    gain = small[step_count]
    driven = gain[None, None, :] * seen.astype(jnp.float32)

    def forward(x):
        out = []
        for k in range(step_count):
            x = split_dot(x, weights[k], False) + x * diag[k][None] + driven[k]
            out.append(x)
        return out

    def backward(e):
        out = []
        for k in range(step_count - 1, -1, -1):
            w = e + driven[k]
            e = split_dot(w, weights[k], True) + w * diag[k][None]
            out.append(e)
        return out

    zeros = jnp.zeros(driven.shape[1:], jnp.float32)
    x_in, e_in = zeros, zeros
    if time_groups <= 8 and time_groups % 2 == 0:
        last = time_groups - 1
        for k in range(last):
            send = lax.cond(
                tm_pos == k,
                lambda x, e: forward(x)[-1],
                lambda x, e: backward(e)[-1],
                x_in,
                e_in,
            )
            pairs = [(k * col_groups + c, (k + 1) * col_groups + c) for c in range(col_groups)]
            pairs += [((last - k) * col_groups + c, (last - k - 1) * col_groups + c) for c in range(col_groups)]
            got = lax.ppermute(send, ("tm", "col"), pairs)
            x_in = jnp.where(tm_pos == k + 1, got, x_in)
            e_in = jnp.where(tm_pos == last - k - 1, got, e_in)
    else:
        def stage(_, carry):
            x, e = carry
            return passed_along(forward(x)[-1], "tm", 1), passed_along(backward(e)[-1], "tm", -1)

        x_in, e_in = lax.fori_loop(0, time_groups - 1, stage, (x_in, e_in))
    xs = forward(x_in)
    es = backward(e_in)
    filtered = jnp.stack(xs)
    correction = jnp.stack([es[step_count - 2 - k] for k in range(step_count - 1)] + [e_in])
    mine = jnp.stack([filtered, filtered + correction])
    parts = [mine[:, :, :, j * cols : (j + 1) * cols] for j in range(col_groups)]

    def pick(options, which):
        out = options[0]
        for j in range(1, col_groups):
            out = jnp.where(which == j, options[j], out)
        return out

    arrived = []
    for shift in range(col_groups):
        piece = pick(parts, (col_pos + shift) % col_groups)
        if shift:
            pairs = [
                (t * col_groups + c, t * col_groups + (c + shift) % col_groups)
                for t in range(time_groups)
                for c in range(col_groups)
            ]
            piece = lax.ppermute(piece, ("tm", "col"), pairs)
        arrived.append(piece)
    got = jnp.stack([pick(arrived, (col_pos - j) % col_groups) for j in range(col_groups)], axis=2)
    got = got.reshape(2, step_count, rows, cols)
    return got[0], got[1]


def solution(mesh):
    return jax.shard_map(
        local,
        mesh=mesh,
        in_specs=(P("tm", None, "col"), P("col"), P("tm", "col"), P("tm", None, "col"), P()),
        out_specs=(P("tm", None, "col"), P("tm", None, "col")),
        check_vma=False,
    )
```

```python
import jax
import jax.numpy as jnp
from jax import lax
from jax.sharding import PartitionSpec as P


def bf16_part(value):
    return lax.reduce_precision(value, exponent_bits=8, mantissa_bits=7)


def split_dot(state, weights, transposed):
    high = bf16_part(state)
    low = state - high
    both = jnp.concatenate([high, low], axis=0).astype(jnp.bfloat16)
    contract = 1 if transposed else 0
    prod = lax.dot_general(
        both, weights, (((1,), (contract,)), ((), ())), preferred_element_type=jnp.float32
    )
    rows = state.shape[0]
    return prod[:rows] + prod[rows:]


def three_pieces(value):
    high = bf16_part(value)
    rest = value - high
    mid = bf16_part(rest)
    return jnp.stack([high, mid, rest - mid]).astype(jnp.bfloat16)


def passed_along(shard, axis, by):
    length = lax.axis_size(axis)
    pairs = [(i, i + by) for i in range(length) if 0 <= i + by < length]
    return lax.ppermute(shard, axis, pairs)


def local(observed, input_gain, persist, coupling, pattern):
    step_count, rows, cols = observed.shape
    state_width = coupling.shape[1]
    block_count = pattern.shape[0]
    block_size = state_width // block_count
    time_groups = lax.axis_size("tm")
    col_groups = lax.axis_size("col")
    own_rows = rows // col_groups
    tm_pos = lax.axis_index("tm")

    col_pos = lax.axis_index("col")
    small = jnp.concatenate([persist, input_gain[None]], axis=0)
    small_rows = 3 * (step_count + 1)
    small_pad = -small_rows % 16
    small_pieces = jnp.pad(three_pieces(small).reshape(small_rows, cols), ((0, small_pad), (0, 0)))
    coupling_rows = coupling.reshape(step_count * state_width, cols)
    seen_parts = observed.reshape(step_count, col_groups, own_rows, cols).transpose(1, 0, 2, 3)
    seen_parts = seen_parts.reshape(col_groups, step_count * own_rows, cols)
    chunks = []
    for shift in range(col_groups):
        dest = (col_pos + shift) % col_groups
        seen_d = lax.dynamic_index_in_dim(seen_parts, dest, 0, keepdims=False)
        chunk = jnp.concatenate([coupling_rows, seen_d, small_pieces], axis=0)
        if shift:
            pairs = [
                (t * col_groups + c, t * col_groups + (c + shift) % col_groups)
                for t in range(time_groups)
                for c in range(col_groups)
            ]
            chunk = lax.ppermute(chunk, ("tm", "col"), pairs)
        chunks.append(chunk)
    def from_source(j):
        which = (col_pos - j) % col_groups
        out = chunks[0]
        for shift in range(1, col_groups):
            out = jnp.where(which == shift, chunks[shift], out)
        return out

    sourced = [from_source(j) for j in range(col_groups)]
    n_coupling = step_count * state_width
    n_seen = step_count * own_rows
    mask = jnp.broadcast_to(
        pattern.astype(jnp.bfloat16)[:, None, :, None],
        (block_count, block_size, block_count, block_size),
    ).reshape(state_width, state_width)
    weights = jnp.concatenate(
        [part[:n_coupling].reshape(step_count, state_width, cols) for part in sourced], axis=2
    ) * mask[None]
    seen = jnp.concatenate(
        [part[n_coupling : n_coupling + n_seen].reshape(step_count, own_rows, cols) for part in sourced],
        axis=2,
    )
    small = jnp.concatenate(
        [
            part[n_coupling + n_seen : n_coupling + n_seen + small_rows]
            .astype(jnp.float32)
            .reshape(3, step_count + 1, cols)
            for part in sourced
        ],
        axis=2,
    )
    small = small[0] + small[1] + small[2]
    diag = small[:step_count]
    gain = small[step_count]
    driven = gain[None, None, :] * seen.astype(jnp.float32)

    def forward(x):
        out = []
        for k in range(step_count):
            x = split_dot(x, weights[k], False) + x * diag[k][None] + driven[k]
            out.append(x)
        return out

    def backward(e):
        out = []
        for k in range(step_count - 1, -1, -1):
            w = e + driven[k]
            e = split_dot(w, weights[k], True) + w * diag[k][None]
            out.append(e)
        return out

    zeros = jnp.zeros(driven.shape[1:], jnp.float32)
    x_in, e_in = zeros, zeros
    if time_groups <= 8 and time_groups % 2 == 0:
        last = time_groups - 1
        for k in range(last):
            send = lax.cond(
                tm_pos == k,
                lambda x, e: forward(x)[-1],
                lambda x, e: backward(e)[-1],
                x_in,
                e_in,
            )
            pairs = [(k * col_groups + c, (k + 1) * col_groups + c) for c in range(col_groups)]
            pairs += [((last - k) * col_groups + c, (last - k - 1) * col_groups + c) for c in range(col_groups)]
            got = lax.ppermute(send, ("tm", "col"), pairs)
            x_in = jnp.where(tm_pos == k + 1, got, x_in)
            e_in = jnp.where(tm_pos == last - k - 1, got, e_in)
    else:
        def stage(_, carry):
            x, e = carry
            return passed_along(forward(x)[-1], "tm", 1), passed_along(backward(e)[-1], "tm", -1)

        x_in, e_in = lax.fori_loop(0, time_groups - 1, stage, (x_in, e_in))
    xs = forward(x_in)
    es = backward(e_in)
    filtered = jnp.stack(xs)
    correction = jnp.stack([es[step_count - 2 - k] for k in range(step_count - 1)] + [e_in])
    mine = jnp.stack([filtered, filtered + correction])
    parts = [mine[:, :, :, j * cols : (j + 1) * cols] for j in range(col_groups)]

    def pick(options, which):
        out = options[0]
        for j in range(1, col_groups):
            out = jnp.where(which == j, options[j], out)
        return out

    arrived = []
    for shift in range(col_groups):
        piece = pick(parts, (col_pos + shift) % col_groups)
        if shift:
            pairs = [
                (t * col_groups + c, t * col_groups + (c + shift) % col_groups)
                for t in range(time_groups)
                for c in range(col_groups)
            ]
            piece = lax.ppermute(piece, ("tm", "col"), pairs)
        arrived.append(piece)
    got = jnp.stack([pick(arrived, (col_pos - j) % col_groups) for j in range(col_groups)], axis=2)
    got = got.reshape(2, step_count, rows, cols)
    return got[0], got[1]


def solution(mesh):
    return jax.shard_map(
        local,
        mesh=mesh,
        in_specs=(P("tm", None, "col"), P("col"), P("tm", "col"), P("tm", None, "col"), P()),
        out_specs=(P("tm", None, "col"), P("tm", None, "col")),
        check_vma=False,
    )
```

```python
import jax
import jax.numpy as jnp
from jax import lax
from jax.sharding import PartitionSpec as P


def bf16_part(value):
    return lax.reduce_precision(value, exponent_bits=8, mantissa_bits=7)


def split_dot(state, weights, transposed):
    high = bf16_part(state)
    low = state - high
    both = jnp.concatenate([high, low], axis=0).astype(jnp.bfloat16)
    contract = 1 if transposed else 0
    prod = lax.dot_general(
        both, weights, (((1,), (contract,)), ((), ())), preferred_element_type=jnp.float32
    )
    rows = state.shape[0]
    return prod[:rows] + prod[rows:]


def three_pieces(value):
    high = bf16_part(value)
    rest = value - high
    mid = bf16_part(rest)
    return jnp.stack([high, mid, rest - mid]).astype(jnp.bfloat16)


def passed_along(shard, axis, by):
    length = lax.axis_size(axis)
    pairs = [(i, i + by) for i in range(length) if 0 <= i + by < length]
    return lax.ppermute(shard, axis, pairs)


def local(observed, input_gain, persist, coupling, pattern):
    step_count, rows, cols = observed.shape
    state_width = coupling.shape[1]
    block_count = pattern.shape[0]
    block_size = state_width // block_count
    time_groups = lax.axis_size("tm")
    col_groups = lax.axis_size("col")
    own_rows = rows // col_groups
    tm_pos = lax.axis_index("tm")

    col_pos = lax.axis_index("col")
    small = jnp.concatenate([persist, input_gain[None]], axis=0)
    small_rows = 3 * (step_count + 1)
    small_pad = -small_rows % 16
    small_pieces = jnp.pad(three_pieces(small).reshape(small_rows, cols), ((0, small_pad), (0, 0)))
    coupling_rows = coupling.reshape(step_count * state_width, cols)
    seen_parts = [
        observed[:, d * own_rows : (d + 1) * own_rows, :].reshape(step_count * own_rows, cols)
        for d in range(col_groups)
    ]
    chunks = []
    for shift in range(col_groups):
        dest = (col_pos + shift) % col_groups
        seen_d = seen_parts[0]
        for d in range(1, col_groups):
            seen_d = jnp.where(dest == d, seen_parts[d], seen_d)
        chunk = jnp.concatenate([coupling_rows, seen_d, small_pieces], axis=0)
        if shift:
            pairs = [
                (t * col_groups + c, t * col_groups + (c + shift) % col_groups)
                for t in range(time_groups)
                for c in range(col_groups)
            ]
            chunk = lax.ppermute(chunk, ("tm", "col"), pairs)
        chunks.append(chunk)
    def from_source(j):
        which = (col_pos - j) % col_groups
        out = chunks[0]
        for shift in range(1, col_groups):
            out = jnp.where(which == shift, chunks[shift], out)
        return out

    sourced = [from_source(j) for j in range(col_groups)]
    n_coupling = step_count * state_width
    n_seen = step_count * own_rows
    mask = jnp.broadcast_to(
        pattern.astype(jnp.bfloat16)[:, None, :, None],
        (block_count, block_size, block_count, block_size),
    ).reshape(state_width, state_width)
    weights = jnp.concatenate(
        [part[:n_coupling].reshape(step_count, state_width, cols) for part in sourced], axis=2
    ) * mask[None]
    seen = jnp.concatenate(
        [part[n_coupling : n_coupling + n_seen].reshape(step_count, own_rows, cols) for part in sourced],
        axis=2,
    )
    small = jnp.concatenate(
        [
            part[n_coupling + n_seen : n_coupling + n_seen + small_rows]
            .astype(jnp.float32)
            .reshape(3, step_count + 1, cols)
            for part in sourced
        ],
        axis=2,
    )
    small = small[0] + small[1] + small[2]
    diag = small[:step_count]
    gain = small[step_count]
    driven = gain[None, None, :] * seen.astype(jnp.float32)

    def forward(x):
        out = []
        for k in range(step_count):
            x = split_dot(x, weights[k], False) + x * diag[k][None] + driven[k]
            out.append(x)
        return out

    def backward(e):
        out = []
        for k in range(step_count - 1, -1, -1):
            w = e + driven[k]
            e = split_dot(w, weights[k], True) + w * diag[k][None]
            out.append(e)
        return out

    zeros = jnp.zeros(driven.shape[1:], jnp.float32)
    x_in, e_in = zeros, zeros
    if time_groups <= 8 and time_groups % 2 == 0:
        last = time_groups - 1
        for k in range(last):
            send = lax.cond(
                tm_pos == k,
                lambda x, e: forward(x)[-1],
                lambda x, e: backward(e)[-1],
                x_in,
                e_in,
            )
            pairs = [(k * col_groups + c, (k + 1) * col_groups + c) for c in range(col_groups)]
            pairs += [((last - k) * col_groups + c, (last - k - 1) * col_groups + c) for c in range(col_groups)]
            got = lax.ppermute(send, ("tm", "col"), pairs)
            x_in = jnp.where(tm_pos == k + 1, got, x_in)
            e_in = jnp.where(tm_pos == last - k - 1, got, e_in)
    else:
        def stage(_, carry):
            x, e = carry
            return passed_along(forward(x)[-1], "tm", 1), passed_along(backward(e)[-1], "tm", -1)

        x_in, e_in = lax.fori_loop(0, time_groups - 1, stage, (x_in, e_in))
    xs = forward(x_in)
    es = backward(e_in)
    filtered = jnp.stack(xs)
    correction = jnp.stack([es[step_count - 2 - k] for k in range(step_count - 1)] + [e_in])
    mine = jnp.stack([filtered, filtered + correction])
    parts = [mine[:, :, :, j * cols : (j + 1) * cols] for j in range(col_groups)]

    def pick(options, which):
        out = options[0]
        for j in range(1, col_groups):
            out = jnp.where(which == j, options[j], out)
        return out

    arrived = []
    for shift in range(col_groups):
        piece = pick(parts, (col_pos + shift) % col_groups)
        if shift:
            pairs = [
                (t * col_groups + c, t * col_groups + (c + shift) % col_groups)
                for t in range(time_groups)
                for c in range(col_groups)
            ]
            piece = lax.ppermute(piece, ("tm", "col"), pairs)
        arrived.append(piece)
    got = jnp.stack([pick(arrived, (col_pos - j) % col_groups) for j in range(col_groups)], axis=2)
    got = got.reshape(2, step_count, rows, cols)
    return got[0], got[1]


def solution(mesh):
    return jax.shard_map(
        local,
        mesh=mesh,
        in_specs=(P("tm", None, "col"), P("col"), P("tm", "col"), P("tm", None, "col"), P()),
        out_specs=(P("tm", None, "col"), P("tm", None, "col")),
        check_vma=False,
    )
```

```python
import jax
import jax.numpy as jnp
from jax import lax
from jax.sharding import PartitionSpec as P


def bf16_part(value):
    return lax.reduce_precision(value, exponent_bits=8, mantissa_bits=7)


def split_dot(state, weights, transposed):
    high = bf16_part(state)
    low = state - high
    both = jnp.concatenate([high, low], axis=0).astype(jnp.bfloat16)
    contract = 1 if transposed else 0
    prod = lax.dot_general(
        both, weights, (((1,), (contract,)), ((), ())), preferred_element_type=jnp.float32
    )
    rows = state.shape[0]
    return prod[:rows] + prod[rows:]


def three_pieces(value):
    high = bf16_part(value)
    rest = value - high
    mid = bf16_part(rest)
    return jnp.stack([high, mid, rest - mid]).astype(jnp.bfloat16)


def passed_along(shard, axis, by):
    length = lax.axis_size(axis)
    pairs = [(i, i + by) for i in range(length) if 0 <= i + by < length]
    return lax.ppermute(shard, axis, pairs)


def local(observed, input_gain, persist, coupling, pattern):
    step_count, rows, cols = observed.shape
    state_width = coupling.shape[1]
    block_count = pattern.shape[0]
    block_size = state_width // block_count
    time_groups = lax.axis_size("tm")
    col_groups = lax.axis_size("col")
    own_rows = rows // col_groups
    tm_pos = lax.axis_index("tm")

    col_pos = lax.axis_index("col")
    small = jnp.concatenate([persist, input_gain[None]], axis=0)
    small_rows = 3 * (step_count + 1)
    small_pad = -small_rows % 16
    small_pieces = jnp.pad(three_pieces(small).reshape(small_rows, cols), ((0, small_pad), (0, 0)))
    coupling_rows = coupling.reshape(step_count * state_width, cols)
    seen_parts = observed.reshape(step_count, col_groups, own_rows, cols).transpose(1, 0, 2, 3)
    seen_parts = seen_parts.reshape(col_groups, step_count * own_rows, cols)
    n_coupling = step_count * state_width
    n_seen = step_count * own_rows
    lead = col_groups // 2
    couplings, extras = [], []
    for shift in range(col_groups):
        dest = (col_pos + shift) % col_groups
        seen_d = lax.dynamic_index_in_dim(seen_parts, dest, 0, keepdims=False)
        extra = jnp.concatenate([seen_d, small_pieces], axis=0)
        pairs = [
            (t * col_groups + c, t * col_groups + (c + shift) % col_groups)
            for t in range(time_groups)
            for c in range(col_groups)
        ]
        if shift == 0:
            couplings.append(coupling_rows)
            extras.append(extra)
        elif shift == lead:
            couplings.append(lax.ppermute(coupling_rows, ("tm", "col"), pairs))
            extras.append(lax.ppermute(extra, ("tm", "col"), pairs))
        else:
            chunk = jnp.concatenate([coupling_rows, extra], axis=0)
            chunk = lax.ppermute(chunk, ("tm", "col"), pairs)
            couplings.append(chunk[:n_coupling])
            extras.append(chunk[n_coupling:])

    def from_source(options, j):
        which = (col_pos - j) % col_groups
        out = options[0]
        for shift in range(1, col_groups):
            out = jnp.where(which == shift, options[shift], out)
        return out

    sourced_c = [from_source(couplings, j) for j in range(col_groups)]
    sourced_x = [from_source(extras, j) for j in range(col_groups)]
    mask = jnp.broadcast_to(
        pattern.astype(jnp.bfloat16)[:, None, :, None],
        (block_count, block_size, block_count, block_size),
    ).reshape(state_width, state_width)
    weights = jnp.concatenate(
        [part.reshape(step_count, state_width, cols) for part in sourced_c], axis=2
    ) * mask[None]
    seen = jnp.concatenate(
        [part[:n_seen].reshape(step_count, own_rows, cols) for part in sourced_x],
        axis=2,
    )
    small = jnp.concatenate(
        [
            part[n_seen : n_seen + small_rows]
            .astype(jnp.float32)
            .reshape(3, step_count + 1, cols)
            for part in sourced_x
        ],
        axis=2,
    )
    small = small[0] + small[1] + small[2]
    diag = small[:step_count]
    gain = small[step_count]
    driven = gain[None, None, :] * seen.astype(jnp.float32)

    def forward(x):
        out = []
        for k in range(step_count):
            x = split_dot(x, weights[k], False) + x * diag[k][None] + driven[k]
            out.append(x)
        return out

    def backward(e):
        out = []
        for k in range(step_count - 1, -1, -1):
            w = e + driven[k]
            e = split_dot(w, weights[k], True) + w * diag[k][None]
            out.append(e)
        return out

    zeros = jnp.zeros(driven.shape[1:], jnp.float32)
    x_in, e_in = zeros, zeros
    if time_groups <= 8 and time_groups % 2 == 0:
        last = time_groups - 1
        for k in range(last):
            send = lax.cond(
                tm_pos == k,
                lambda x, e: forward(x)[-1],
                lambda x, e: backward(e)[-1],
                x_in,
                e_in,
            )
            pairs = [(k * col_groups + c, (k + 1) * col_groups + c) for c in range(col_groups)]
            pairs += [((last - k) * col_groups + c, (last - k - 1) * col_groups + c) for c in range(col_groups)]
            got = lax.ppermute(send, ("tm", "col"), pairs)
            x_in = jnp.where(tm_pos == k + 1, got, x_in)
            e_in = jnp.where(tm_pos == last - k - 1, got, e_in)
    else:
        def stage(_, carry):
            x, e = carry
            return passed_along(forward(x)[-1], "tm", 1), passed_along(backward(e)[-1], "tm", -1)

        x_in, e_in = lax.fori_loop(0, time_groups - 1, stage, (x_in, e_in))
    xs = forward(x_in)
    es = backward(e_in)
    filtered = jnp.stack(xs)
    correction = jnp.stack([es[step_count - 2 - k] for k in range(step_count - 1)] + [e_in])
    mine = jnp.stack([filtered, filtered + correction])
    parts = [mine[:, :, :, j * cols : (j + 1) * cols] for j in range(col_groups)]

    def pick(options, which):
        out = options[0]
        for j in range(1, col_groups):
            out = jnp.where(which == j, options[j], out)
        return out

    arrived = []
    for shift in range(col_groups):
        piece = pick(parts, (col_pos + shift) % col_groups)
        if shift:
            pairs = [
                (t * col_groups + c, t * col_groups + (c + shift) % col_groups)
                for t in range(time_groups)
                for c in range(col_groups)
            ]
            piece = lax.ppermute(piece, ("tm", "col"), pairs)
        arrived.append(piece)
    got = jnp.stack([pick(arrived, (col_pos - j) % col_groups) for j in range(col_groups)], axis=2)
    got = got.reshape(2, step_count, rows, cols)
    return got[0], got[1]


def solution(mesh):
    return jax.shard_map(
        local,
        mesh=mesh,
        in_specs=(P("tm", None, "col"), P("col"), P("tm", "col"), P("tm", None, "col"), P()),
        out_specs=(P("tm", None, "col"), P("tm", None, "col")),
        check_vma=False,
    )
```

```python
import jax
import jax.numpy as jnp
from jax import lax
from jax.sharding import PartitionSpec as P


def bf16_part(value):
    return lax.reduce_precision(value, exponent_bits=8, mantissa_bits=7)


def split_dot(state, weights, transposed):
    high = bf16_part(state)
    low = state - high
    both = jnp.concatenate([high, low], axis=0).astype(jnp.bfloat16)
    contract = 1 if transposed else 0
    prod = lax.dot_general(
        both, weights, (((1,), (contract,)), ((), ())), preferred_element_type=jnp.float32
    )
    rows = state.shape[0]
    return prod[:rows] + prod[rows:]


def three_pieces(value):
    high = bf16_part(value)
    rest = value - high
    mid = bf16_part(rest)
    return jnp.stack([high, mid, rest - mid]).astype(jnp.bfloat16)


def passed_along(shard, axis, by):
    length = lax.axis_size(axis)
    pairs = [(i, i + by) for i in range(length) if 0 <= i + by < length]
    return lax.ppermute(shard, axis, pairs)


def local(observed, input_gain, persist, coupling, pattern):
    step_count, rows, cols = observed.shape
    state_width = coupling.shape[1]
    block_count = pattern.shape[0]
    block_size = state_width // block_count
    time_groups = lax.axis_size("tm")
    col_groups = lax.axis_size("col")
    own_rows = rows // col_groups
    tm_pos = lax.axis_index("tm")

    col_pos = lax.axis_index("col")
    small = jnp.concatenate([persist, input_gain[None]], axis=0)
    small_rows = 3 * (step_count + 1)
    small_pad = -small_rows % 16
    small_pieces = jnp.pad(three_pieces(small).reshape(small_rows, cols), ((0, small_pad), (0, 0)))
    coupling_rows = coupling.reshape(step_count * state_width, cols)
    seen_parts = observed.reshape(step_count, col_groups, own_rows, cols).transpose(1, 0, 2, 3)
    seen_parts = seen_parts.reshape(col_groups, step_count * own_rows, cols)
    n_seen = step_count * own_rows
    couplings, extras = [], []
    for shift in range(col_groups):
        dest = (col_pos + shift) % col_groups
        seen_d = lax.dynamic_index_in_dim(seen_parts, dest, 0, keepdims=False)
        extra = jnp.concatenate([seen_d, small_pieces], axis=0)
        pairs = [
            (t * col_groups + c, t * col_groups + (c + shift) % col_groups)
            for t in range(time_groups)
            for c in range(col_groups)
        ]
        if shift == 0:
            couplings.append(coupling_rows)
            extras.append(extra)
        else:
            couplings.append(lax.ppermute(coupling_rows, ("tm", "col"), pairs))
            extras.append(lax.ppermute(extra, ("tm", "col"), pairs))

    def from_source(options, j):
        which = (col_pos - j) % col_groups
        out = options[0]
        for shift in range(1, col_groups):
            out = jnp.where(which == shift, options[shift], out)
        return out

    sourced_c = [from_source(couplings, j) for j in range(col_groups)]
    sourced_x = [from_source(extras, j) for j in range(col_groups)]
    mask = jnp.broadcast_to(
        pattern.astype(jnp.bfloat16)[:, None, :, None],
        (block_count, block_size, block_count, block_size),
    ).reshape(state_width, state_width)
    weights = jnp.concatenate(
        [part.reshape(step_count, state_width, cols) for part in sourced_c], axis=2
    ) * mask[None]
    seen = jnp.concatenate(
        [part[:n_seen].reshape(step_count, own_rows, cols) for part in sourced_x],
        axis=2,
    )
    small = jnp.concatenate(
        [
            part[n_seen : n_seen + small_rows]
            .astype(jnp.float32)
            .reshape(3, step_count + 1, cols)
            for part in sourced_x
        ],
        axis=2,
    )
    small = small[0] + small[1] + small[2]
    diag = small[:step_count]
    gain = small[step_count]
    driven = gain[None, None, :] * seen.astype(jnp.float32)

    def forward(x):
        out = []
        for k in range(step_count):
            x = split_dot(x, weights[k], False) + x * diag[k][None] + driven[k]
            out.append(x)
        return out

    def backward(e):
        out = []
        for k in range(step_count - 1, -1, -1):
            w = e + driven[k]
            e = split_dot(w, weights[k], True) + w * diag[k][None]
            out.append(e)
        return out

    zeros = jnp.zeros(driven.shape[1:], jnp.float32)
    x_in, e_in = zeros, zeros
    if time_groups <= 8 and time_groups % 2 == 0:
        last = time_groups - 1
        for k in range(last):
            send = lax.cond(
                tm_pos == k,
                lambda x, e: forward(x)[-1],
                lambda x, e: backward(e)[-1],
                x_in,
                e_in,
            )
            pairs = [(k * col_groups + c, (k + 1) * col_groups + c) for c in range(col_groups)]
            pairs += [((last - k) * col_groups + c, (last - k - 1) * col_groups + c) for c in range(col_groups)]
            got = lax.ppermute(send, ("tm", "col"), pairs)
            x_in = jnp.where(tm_pos == k + 1, got, x_in)
            e_in = jnp.where(tm_pos == last - k - 1, got, e_in)
    else:
        def stage(_, carry):
            x, e = carry
            return passed_along(forward(x)[-1], "tm", 1), passed_along(backward(e)[-1], "tm", -1)

        x_in, e_in = lax.fori_loop(0, time_groups - 1, stage, (x_in, e_in))
    xs = forward(x_in)
    es = backward(e_in)
    filtered = jnp.stack(xs)
    correction = jnp.stack([es[step_count - 2 - k] for k in range(step_count - 1)] + [e_in])
    mine = jnp.stack([filtered, filtered + correction])
    parts = [mine[:, :, :, j * cols : (j + 1) * cols] for j in range(col_groups)]

    def pick(options, which):
        out = options[0]
        for j in range(1, col_groups):
            out = jnp.where(which == j, options[j], out)
        return out

    arrived = []
    for shift in range(col_groups):
        piece = pick(parts, (col_pos + shift) % col_groups)
        if shift:
            pairs = [
                (t * col_groups + c, t * col_groups + (c + shift) % col_groups)
                for t in range(time_groups)
                for c in range(col_groups)
            ]
            piece = lax.ppermute(piece, ("tm", "col"), pairs)
        arrived.append(piece)
    got = jnp.stack([pick(arrived, (col_pos - j) % col_groups) for j in range(col_groups)], axis=2)
    got = got.reshape(2, step_count, rows, cols)
    return got[0], got[1]


def solution(mesh):
    return jax.shard_map(
        local,
        mesh=mesh,
        in_specs=(P("tm", None, "col"), P("col"), P("tm", "col"), P("tm", None, "col"), P()),
        out_specs=(P("tm", None, "col"), P("tm", None, "col")),
        check_vma=False,
    )
```
